128 devices in a mesh: ctx: 32 (over x, y, core), head: 4 (over z).
Axes of the slice: x: 4, y: 4, z: 4, core: 2. Of those that a mesh axis runs over, the one named last changes fastest.
Arguments:
- queries: bfloat16 [32768, 4096], P('ctx', 'head'), may hold values from -4.5 to 4.5
- keys: bfloat16 [32768, 4096], P('ctx', 'head'), may hold values from -6 to 6
- values: bfloat16 [32768, 4096], P('ctx', 'head'), may hold values from -5.5 to 5.5
- row_target: int32 [32768], replicated, may hold values from 0 to 32767, as said below
- seg_doc: int32 [32], replicated, may hold values from 0 to 3, as said below
- mem_gate: float32 [32], P('head'), may hold values from -2 to 2
- out_weight: bfloat16 [4096, 4096], P(None, 'head'), may hold values from -0.09375 to 0.09375
Outputs:
- layer_out: bfloat16 [32768, 4096], P('ctx', 'head')
The draws below stay inside these ranges and needn't reach their ends.
Inputs may be any that keep to these rules, and one draw needn't show every extreme that they name: `row_target`: a permutation of the token indices; the rows of one ctx shard of the loader order hold at most 48 tokens of any one segment, and exactly 48 of some. `seg_doc`: never falling along the segments, every document present with one or more segments.
All inputs are finite; a program needn't handle non-finite values.
Results may differ from the reference program's by a relative error of at most 0.0051.
Values may be sent and summed in bfloat16 or wider, within the bound.
No kernel may reach another device: no remote copies, remote signals or barrier semaphores. Data moves between devices by JAX's collectives and lax.ppermute only.
A program may use at most 128 MiB of HBM per device.

```python
import math
import jax
import jax.numpy as jnp
from jax import lax

D = 4096
HEADS = 32
DH = 128
SEG = 1024
DOCS = 4
TOKENS = 32768
N_CTX = 32


def one_loader(row_counts, starts, offsets, loader_key):
    indices = jnp.arange(N_CTX, dtype=jnp.int32)
    owners = jnp.repeat(indices, row_counts, total_repeat_length=SEG)
    within = jnp.arange(SEG, dtype=jnp.int32) - offsets[owners] + starts[owners]
    shuffle = jax.random.permutation(loader_key, SEG)
    return (owners[shuffle], within[shuffle])


def owner_order(owner_key):
    return jax.random.permutation(owner_key, SEG).astype(jnp.int32)


def target_table(key):
    base = jax.random.fold_in(key, 101)
    pair_rows = SEG // N_CTX
    half = N_CTX // 2
    levels = jnp.concatenate([jnp.full((half,), pair_rows + pair_rows // 2, jnp.int32), jnp.full((half,), pair_rows // 2, jnp.int32)])
    levels = levels[jax.random.permutation(jax.random.fold_in(base, 1), N_CTX)]
    indices = jnp.arange(N_CTX, dtype=jnp.int32)
    counts = levels[(indices[None, :] - indices[:, None]) % N_CTX]
    before_loader = jnp.cumsum(counts, axis=0) - counts
    before_owner = jnp.cumsum(counts, axis=1) - counts
    loader_keys = jax.random.split(jax.random.fold_in(base, 2), N_CTX)
    owners, within = jax.vmap(one_loader)(counts, before_loader, before_owner, loader_keys)
    owner_keys = jax.random.split(jax.random.fold_in(base, 3), N_CTX)
    places = jax.vmap(owner_order)(owner_keys)
    return (owners * SEG + places[owners, within]).reshape(-1).astype(jnp.int32)


def source_rows(key):
    target = target_table(key)
    return target


def draw_row_target(key, part):
    return target_table(key)


def draw_seg_doc(key, part):
    cut_key = jax.random.fold_in(key, 707)
    cuts = jnp.sort(jax.random.permutation(cut_key, N_CTX - 1)[:DOCS - 1].astype(jnp.int32)) + 1
    indices = jnp.arange(N_CTX, dtype=jnp.int32)
    return jnp.sum((indices[:, None] >= cuts[None, :]).astype(jnp.int32), axis=1).astype(jnp.int32)


def draw_queries(key, part):
    own_key = jax.random.fold_in(key, 303)
    field = jnp.clip(jax.random.normal(own_key, (TOKENS, HEADS * DH), jnp.float32), -3.0, 3.0)
    return field.astype(jnp.bfloat16)


def draw_keys(key, part):
    target = source_rows(key)
    own_key = jax.random.fold_in(key, 404)
    scale_key = jax.random.fold_in(key, 405)
    seg_scale = jnp.exp(jax.random.uniform(scale_key, (N_CTX,), jnp.float32, math.log(0.3), math.log(2.4)))
    row_scale = seg_scale[target // SEG]
    noise = jnp.clip(jax.random.normal(own_key, (TOKENS, HEADS * DH), jnp.float32), -2.5, 2.5)
    field = noise * row_scale[:, None]
    return field.astype(jnp.bfloat16)


def draw_values(key, part):
    target = source_rows(key)
    own_key = jax.random.fold_in(key, 505)
    offset_key = jax.random.fold_in(key, 506)
    offsets = jax.random.uniform(offset_key, (N_CTX, HEADS * DH), jnp.float32, -1.5, 1.5)
    noise = jnp.clip(jax.random.normal(own_key, (TOKENS, HEADS * DH), jnp.float32), -3.0, 3.0)
    field = noise + offsets[target // SEG]
    return field.astype(jnp.bfloat16)


def block_levels(rng, shape, cuts, smallest, largest):
    gain, own = 1.0, jax.random.fold_in(rng, 6)
    for axis_at, parts in cuts:
        steps = jnp.exp(jax.random.uniform(jax.random.fold_in(own, axis_at), (parts,), jnp.float32, smallest / len(cuts), largest / len(cuts)))
        gain = gain * jnp.repeat(steps, shape[axis_at] // parts).reshape([-1 if axis == axis_at else 1 for axis in range(len(shape))])
    return gain


def normal_values(key, dims, spread, bound, cuts=(), kind=jnp.bfloat16):
    loudness = block_levels(key, dims, cuts, -0.22, 0.18) if cuts else 1.0
    values = jax.random.normal(key, dims, jnp.float32) * spread * loudness
    return jnp.minimum(jnp.maximum(values, -bound), bound).astype(kind)


def setup_inputs(seed: int = 0) -> dict:
    streams_of = jax.random.split(jax.random.key(seed), 8)
    return {
        "queries": draw_queries(jax.random.fold_in(streams_of[7], 71), 0),
        "keys": draw_keys(jax.random.fold_in(streams_of[7], 71), 0),
        "values": draw_values(jax.random.fold_in(streams_of[7], 71), 0),
        "row_target": draw_row_target(jax.random.fold_in(streams_of[7], 71), 0),
        "seg_doc": draw_seg_doc(jax.random.fold_in(streams_of[7], 71), 0),
        "mem_gate": jnp.clip(jax.random.uniform(streams_of[5], (HEADS,), jnp.float32, -2.0, 2.0) * block_levels(streams_of[5], (HEADS,), ((0, 4),), -0.4, 0.0), -2.0, 2.0),
        "out_weight": normal_values(streams_of[6], (HEADS * DH, D), (HEADS * DH) ** -0.5, 0.09375, ((1, 4),)),
    }


def feature(inputs):
    return jax.nn.elu(inputs) + 1.0


def reference(queries, keys, values, row_target, seg_doc, mem_gate, out_weight):
    highest = lax.Precision.HIGHEST
    total_rows = row_target.shape[0]
    source = jnp.zeros((total_rows,), jnp.int32).at[row_target].set(jnp.arange(total_rows, dtype=jnp.int32))
    query_tok = queries[source].reshape(N_CTX, SEG, HEADS, DH)
    key_tok = keys[source].reshape(N_CTX, SEG, HEADS, DH)
    value_tok = values[source].reshape(N_CTX, SEG, HEADS, DH)

    def memory_terms(items):
        key_seg, value_seg = items
        key_feat = feature(key_seg.astype(jnp.float32))
        matrix = jnp.einsum("khd,khe->hde", key_feat, value_seg.astype(jnp.float32), precision=highest)
        return matrix, jnp.sum(key_feat, axis=0)

    delta_m, delta_z = lax.map(memory_terms, (key_tok, value_tok))
    indices = jnp.arange(N_CTX)
    earlier = ((seg_doc[:, None] == seg_doc[None, :]) & (indices[None, :] < indices[:, None])).astype(jnp.float32)
    mem_m = jnp.einsum("ij,jhde->ihde", earlier, delta_m, precision=highest)
    mem_z = jnp.einsum("ij,jhd->ihd", earlier, delta_z, precision=highest)
    gate_value = jax.nn.sigmoid(mem_gate)[None, :, None]
    position = jnp.arange(SEG)
    causal = position[:, None] >= position[None, :]

    def one_segment(items):
        query_seg, key_seg, value_seg, matrix, normal = items
        query_float = query_seg.astype(jnp.float32)
        scores = jnp.einsum("qhd,khd->hqk", query_float, key_seg.astype(jnp.float32), precision=highest) * (DH ** -0.5)
        scores = jnp.where(causal[None], scores, -1e30)
        row_max = jnp.max(scores, axis=-1, keepdims=True)
        weights = jnp.exp(scores - row_max)
        probabilities = (weights / jnp.sum(weights, axis=-1, keepdims=True)).astype(jnp.bfloat16)
        probabilities = lax.optimization_barrier(probabilities)
        local_out = jnp.einsum("hqk,khd->qhd", probabilities.astype(jnp.float32), value_seg.astype(jnp.float32), precision=highest)
        query_feat = feature(query_float)
        numerator = jnp.einsum("qhd,hde->qhe", query_feat, matrix, precision=highest)
        denominator = jnp.einsum("qhd,hd->qh", query_feat, normal, precision=highest)
        recalled = numerator / jnp.maximum(denominator, 1.0)[..., None]
        mixed = gate_value * recalled + (1.0 - gate_value) * local_out
        return mixed.astype(jnp.bfloat16).reshape(SEG, HEADS * DH)

    combined = lax.map(one_segment, (query_tok, key_tok, value_tok, mem_m, mem_z)).reshape(N_CTX * SEG, HEADS * DH)
    return jnp.dot(combined[row_target], out_weight, preferred_element_type=jnp.float32).astype(jnp.bfloat16)
```

```python
import jax
import jax.numpy as jnp
from jax import lax
from jax.sharding import PartitionSpec as P


def feature(inputs):
    return jax.nn.elu(inputs) + 1.0


def per_device(queries, keys, values, row_target, seg_doc, mem_gate, out_weight):
    highest = lax.Precision.HIGHEST
    f32, bf16 = jnp.float32, jnp.bfloat16
    n = lax.axis_size("ctx")
    me = lax.axis_index("ctx")
    seg, width = queries.shape
    heads = mem_gate.shape[0]
    dh = width // heads
    cap = seg // n + (seg // n) // 2
    slots = n * cap

    targets = row_target.reshape(n, seg)
    r_idx = jnp.arange(seg, dtype=jnp.int32)
    o_idx = jnp.arange(n, dtype=jnp.int32)
    s_idx = jnp.arange(slots, dtype=jnp.int32)
    w_idx = jnp.arange(cap, dtype=jnp.int32)
    lower = (r_idx[None, :] < r_idx[:, None]).astype(bf16)

    mine = lax.dynamic_index_in_dim(targets, me, 0, keepdims=False)
    owner = mine // seg
    match = (owner[:, None] == o_idx[None, :]).astype(bf16)
    before = jnp.dot(lower, match, preferred_element_type=f32)
    within = jnp.sum(jnp.where(match > 0, before, 0.0), axis=1).astype(jnp.int32)
    send_slot = owner * cap + within
    slot_row = jnp.sum(
        jnp.where(send_slot[None, :] == s_idx[:, None], r_idx[None, :], 0), axis=1
    )

    arrived = (targets // seg) == me
    rank = jnp.dot(arrived.astype(bf16), lower.T, preferred_element_type=f32).astype(jnp.int32)
    hit = arrived[:, None, :] & (rank[:, None, :] == w_idx[None, :, None])
    pslot = jnp.sum(jnp.where(hit, (targets % seg)[:, None, :], 0), axis=2).reshape(slots)
    count = jnp.sum(arrived.astype(jnp.int32), axis=1)
    valid = (w_idx[None, :] < count[:, None]).reshape(slots)
    tok_slot = jnp.sum(
        jnp.where((pslot[None, :] == r_idx[:, None]) & valid[None, :], s_idx[None, :], 0),
        axis=1,
    )

    def dispatch(source):
        buffer = jnp.take(source, slot_row, axis=0, mode="clip").reshape(n, cap, width)
        got = lax.all_to_all(buffer, "ctx", 0, 0, tiled=True).reshape(slots, width)
        return jnp.take(got, tok_slot, axis=0, mode="clip").reshape(seg, heads, dh)

    key_heads = dispatch(keys)
    value_heads = dispatch(values)
    query_heads = dispatch(queries)

    key_feat = feature(key_heads.astype(f32))
    delta_m = jnp.einsum(
        "khd,khe->hde", key_feat, value_heads.astype(f32), precision=highest
    )
    delta_z = jnp.sum(key_feat, axis=0)
    delta = jnp.concatenate([delta_m, delta_z[:, None, :]], axis=1)
    doc = seg_doc[me]
    start = jnp.min(jnp.where(seg_doc == doc, o_idx, n))
    total = delta
    step = 1
    while step < n:
        perm = [(j, j + step) for j in range(n - step)]
        got = lax.ppermute(total, "ctx", perm)
        total = total + jnp.where(me - step >= start, got, jnp.zeros_like(got))
        step *= 2
    memory = total - delta
    mem_m = memory[:, :dh, :]
    mem_z = memory[:, dh, :]

    score_scale = dh ** (-0.5)
    scores = jnp.einsum(
        "qhd,khd->hqk", query_heads, key_heads, preferred_element_type=f32
    ) * score_scale
    causal = r_idx[:, None] >= r_idx[None, :]
    scores = jnp.where(causal[None], scores, -1e30)
    row_max = jnp.max(scores, axis=-1, keepdims=True)
    weights = jnp.exp(scores - row_max)
    probabilities = (weights / jnp.sum(weights, axis=-1, keepdims=True)).astype(bf16)
    local_out = jnp.einsum(
        "hqk,khd->qhd", probabilities, value_heads, preferred_element_type=f32
    )

    query_feat = feature(query_heads.astype(f32))
    numerator = jnp.einsum("qhd,hde->qhe", query_feat, mem_m, precision=highest)
    denominator = jnp.einsum("qhd,hd->qh", query_feat, mem_z, precision=highest)
    recalled = numerator / jnp.maximum(denominator, 1.0)[..., None]
    gate_value = jax.nn.sigmoid(mem_gate)[None, :, None]
    combined = (
        (gate_value * recalled + (1.0 - gate_value) * local_out)
        .astype(bf16)
        .reshape(seg, width)
    )

    outgoing = jnp.take(combined, pslot, axis=0, mode="clip").reshape(n, cap, width)
    incoming = lax.all_to_all(outgoing, "ctx", 0, 0, tiled=True).reshape(slots, width)
    rows = jnp.take(incoming, send_slot, axis=0, mode="clip")
    gathered = lax.all_gather(rows, "head", axis=1, tiled=True)
    summed = jnp.dot(gathered, out_weight, preferred_element_type=f32)
    return summed.astype(bf16)


def solution(mesh):
    return jax.shard_map(
        per_device,
        mesh=mesh,
        in_specs=(
            P("ctx", "head"),
            P("ctx", "head"),
            P("ctx", "head"),
            P(),
            P(),
            P("head"),
            P(None, "head"),
        ),
        out_specs=P("ctx", "head"),
        check_vma=False,
    )
```

```python
import jax
import jax.numpy as jnp
from jax import lax
from jax.sharding import PartitionSpec as P


def feature(inputs):
    return jax.nn.elu(inputs) + 1.0


def per_device(queries, keys, values, row_target, seg_doc, mem_gate, out_weight):
    highest = lax.Precision.HIGHEST
    f32, bf16 = jnp.float32, jnp.bfloat16
    n = lax.axis_size("ctx")
    me = lax.axis_index("ctx")
    seg, width = queries.shape
    heads = mem_gate.shape[0]
    dh = width // heads
    cap = seg // n + (seg // n) // 2
    slots = n * cap

    targets = row_target.reshape(n, seg)
    r_idx = jnp.arange(seg, dtype=jnp.int32)
    o_idx = jnp.arange(n, dtype=jnp.int32)
    s_idx = jnp.arange(slots, dtype=jnp.int32)
    w_idx = jnp.arange(cap, dtype=jnp.int32)
    lower = (r_idx[None, :] < r_idx[:, None]).astype(bf16)

    mine = lax.dynamic_index_in_dim(targets, me, 0, keepdims=False)
    owner = mine // seg
    match = (owner[:, None] == o_idx[None, :]).astype(bf16)
    before = jnp.dot(lower, match, preferred_element_type=f32)
    within = jnp.sum(jnp.where(match > 0, before, 0.0), axis=1).astype(jnp.int32)
    send_slot = owner * cap + within
    slot_row = jnp.sum(
        jnp.where(send_slot[None, :] == s_idx[:, None], r_idx[None, :], 0), axis=1
    )

    arrived = (targets // seg) == me
    rank = jnp.dot(arrived.astype(bf16), lower.T, preferred_element_type=f32).astype(jnp.int32)
    hit = arrived[:, None, :] & (rank[:, None, :] == w_idx[None, :, None])
    pslot = jnp.sum(jnp.where(hit, (targets % seg)[:, None, :], 0), axis=2).reshape(slots)
    count = jnp.sum(arrived.astype(jnp.int32), axis=1)
    valid = (w_idx[None, :] < count[:, None]).reshape(slots)
    tok_slot = jnp.sum(
        jnp.where((pslot[None, :] == r_idx[:, None]) & valid[None, :], s_idx[None, :], 0),
        axis=1,
    )

    def dispatch(source):
        buffer = jnp.take(source, slot_row, axis=0, mode="clip").reshape(n, cap, width)
        got = lax.all_to_all(buffer, "ctx", 0, 0, tiled=True).reshape(slots, width)
        return jnp.take(got, tok_slot, axis=0, mode="clip").reshape(seg, heads, dh)

    key_heads = dispatch(keys)
    value_heads = dispatch(values)
    query_heads = dispatch(queries)

    key_feat = feature(key_heads.astype(f32))
    delta_m = jnp.einsum(
        "khd,khe->hde", key_feat, value_heads.astype(f32), precision=highest
    )
    delta_z = jnp.sum(key_feat, axis=0)
    delta = jnp.concatenate([delta_m, delta_z[:, None, :]], axis=1)
    doc = seg_doc[me]
    start = jnp.min(jnp.where(seg_doc == doc, o_idx, n))
    score_scale = dh ** (-0.5)
    causal = r_idx[:, None] >= r_idx[None, :]

    def local_attention(query_part, key_part, value_part):
        scores = jnp.einsum(
            "qhd,khd->hqk", query_part, key_part, preferred_element_type=f32
        ) * score_scale
        scores = jnp.where(causal[None], scores, -1e30)
        row_max = jnp.max(scores, axis=-1, keepdims=True)
        weights = jnp.exp(scores - row_max)
        probabilities = (weights / jnp.sum(weights, axis=-1, keepdims=True)).astype(bf16)
        return jnp.einsum(
            "hqk,khd->qhd", probabilities, value_part, preferred_element_type=f32
        )

    shifts = []
    step = 1
    while step < n:
        shifts.append(step)
        step *= 2
    cuts = [round(heads * i / len(shifts)) for i in range(len(shifts) + 1)]
    pieces = []
    total = delta
    for k, step in enumerate(shifts):
        lo, hi = cuts[k], cuts[k + 1]
        total, operands = lax.optimization_barrier(
            (total, (query_heads[:, lo:hi], key_heads[:, lo:hi], value_heads[:, lo:hi]))
        )
        perm = [(j, j + step) for j in range(n - step)]
        got = lax.ppermute(total, "ctx", perm)
        piece = local_attention(*operands)
        got, piece = lax.optimization_barrier((got, piece))
        pieces.append(piece)
        total = total + jnp.where(me - step >= start, got, jnp.zeros_like(got))
    local_out = jnp.concatenate(pieces, axis=1)
    memory = total - delta
    mem_m = memory[:, :dh, :]
    mem_z = memory[:, dh, :]

    query_feat = feature(query_heads.astype(f32))
    numerator = jnp.einsum("qhd,hde->qhe", query_feat, mem_m, precision=highest)
    denominator = jnp.einsum("qhd,hd->qh", query_feat, mem_z, precision=highest)
    recalled = numerator / jnp.maximum(denominator, 1.0)[..., None]
    gate_value = jax.nn.sigmoid(mem_gate)[None, :, None]
    combined = (
        (gate_value * recalled + (1.0 - gate_value) * local_out)
        .astype(bf16)
        .reshape(seg, width)
    )

    head_count = lax.axis_size("head")
    out_cols = out_weight.shape[1]
    halves = 2
    half = width // halves
    weight_parts = out_weight.reshape(head_count, halves, half, out_cols)
    summed = None
    for p in range(halves):
        outgoing = jnp.take(
            combined[:, p * half:(p + 1) * half], pslot, axis=0, mode="clip"
        ).reshape(n, cap, half)
        incoming = lax.all_to_all(outgoing, "ctx", 0, 0, tiled=True).reshape(slots, half)
        rows = jnp.take(incoming, send_slot, axis=0, mode="clip")
        gathered = lax.all_gather(rows, "head", axis=1, tiled=True)
        part = jnp.dot(
            gathered,
            weight_parts[:, p].reshape(head_count * half, out_cols),
            preferred_element_type=f32,
        )
        summed = part if summed is None else summed + part
    return summed.astype(bf16)


def solution(mesh):
    return jax.shard_map(
        per_device,
        mesh=mesh,
        in_specs=(
            P("ctx", "head"),
            P("ctx", "head"),
            P("ctx", "head"),
            P(),
            P(),
            P("head"),
            P(None, "head"),
        ),
        out_specs=P("ctx", "head"),
        check_vma=False,
    )
```

```python
import jax
import jax.numpy as jnp
from jax import lax
from jax.sharding import PartitionSpec as P


def feature(inputs):
    return jax.nn.elu(inputs) + 1.0


def per_device(queries, keys, values, row_target, seg_doc, mem_gate, out_weight):
    highest = lax.Precision.HIGHEST
    f32, bf16 = jnp.float32, jnp.bfloat16
    n = lax.axis_size("ctx")
    me = lax.axis_index("ctx")
    seg, width = queries.shape
    heads = mem_gate.shape[0]
    dh = width // heads
    cap = seg // n + (seg // n) // 2
    slots = n * cap

    targets = row_target.reshape(n, seg)
    r_idx = jnp.arange(seg, dtype=jnp.int32)
    o_idx = jnp.arange(n, dtype=jnp.int32)
    s_idx = jnp.arange(slots, dtype=jnp.int32)
    w_idx = jnp.arange(cap, dtype=jnp.int32)
    lower = (r_idx[None, :] < r_idx[:, None]).astype(bf16)

    mine = lax.dynamic_index_in_dim(targets, me, 0, keepdims=False)
    owner = mine // seg
    match = (owner[:, None] == o_idx[None, :]).astype(bf16)
    before = jnp.dot(lower, match, preferred_element_type=f32)
    within = jnp.sum(jnp.where(match > 0, before, 0.0), axis=1).astype(jnp.int32)
    send_slot = owner * cap + within
    slot_row = jnp.sum(
        jnp.where(send_slot[None, :] == s_idx[:, None], r_idx[None, :], 0), axis=1
    )

    arrived = (targets // seg) == me
    rank = jnp.dot(arrived.astype(bf16), lower.T, preferred_element_type=f32).astype(jnp.int32)
    hit = arrived[:, None, :] & (rank[:, None, :] == w_idx[None, :, None])
    pslot = jnp.sum(jnp.where(hit, (targets % seg)[:, None, :], 0), axis=2).reshape(slots)
    count = jnp.sum(arrived.astype(jnp.int32), axis=1)
    valid = (w_idx[None, :] < count[:, None]).reshape(slots)
    tok_slot = jnp.sum(
        jnp.where((pslot[None, :] == r_idx[:, None]) & valid[None, :], s_idx[None, :], 0),
        axis=1,
    )

    doc = seg_doc[me]
    start = jnp.min(jnp.where(seg_doc == doc, o_idx, n))
    score_scale = dh ** (-0.5)
    causal = r_idx[:, None] >= r_idx[None, :]
    head_count = lax.axis_size("head")
    out_cols = out_weight.shape[1]
    groups = 2
    group_heads = heads // groups
    group_width = width // groups
    weight_parts = out_weight.reshape(head_count, groups, group_width, out_cols)
    gate_all = jax.nn.sigmoid(mem_gate)
    shifts = []
    step = 1
    while step < n:
        shifts.append(step)
        step *= 2
    cuts = [round(group_heads * i / len(shifts)) for i in range(len(shifts) + 1)]

    def dispatch(source, g):
        columns = source[:, g * group_width:(g + 1) * group_width]
        buffer = jnp.take(columns, slot_row, axis=0, mode="clip").reshape(n, cap, group_width)
        got = lax.all_to_all(buffer, "ctx", 0, 0, tiled=True).reshape(slots, group_width)
        return jnp.take(got, tok_slot, axis=0, mode="clip").reshape(seg, group_heads, dh)

    def local_attention(query_part, key_part, value_part):
        scores = jnp.einsum(
            "qhd,khd->hqk", query_part, key_part, preferred_element_type=f32
        ) * score_scale
        scores = jnp.where(causal[None], scores, -1e30)
        row_max = jnp.max(scores, axis=-1, keepdims=True)
        weights = jnp.exp(scores - row_max)
        probabilities = (weights / jnp.sum(weights, axis=-1, keepdims=True)).astype(bf16)
        return jnp.einsum(
            "hqk,khd->qhd", probabilities, value_part, preferred_element_type=f32
        )

    def one_group(g):
        key_heads = dispatch(keys, g)
        value_heads = dispatch(values, g)
        query_heads = dispatch(queries, g)

        key_feat = feature(key_heads.astype(f32))
        delta_m = jnp.einsum(
            "khd,khe->hde", key_feat, value_heads.astype(f32), precision=highest
        )
        delta_z = jnp.sum(key_feat, axis=0)
        delta = jnp.concatenate([delta_m, delta_z[:, None, :]], axis=1)

        pieces = []
        total = delta
        for k, step in enumerate(shifts):
            lo, hi = cuts[k], cuts[k + 1]
            total, operands = lax.optimization_barrier(
                (total, (query_heads[:, lo:hi], key_heads[:, lo:hi], value_heads[:, lo:hi]))
            )
            perm = [(j, j + step) for j in range(n - step)]
            got = lax.ppermute(total, "ctx", perm)
            if hi > lo:
                piece = local_attention(*operands)
                got, piece = lax.optimization_barrier((got, piece))
                pieces.append(piece)
            total = total + jnp.where(me - step >= start, got, jnp.zeros_like(got))
        local_out = jnp.concatenate(pieces, axis=1)
        memory = total - delta
        mem_m = memory[:, :dh, :]
        mem_z = memory[:, dh, :]

        query_feat = feature(query_heads.astype(f32))
        numerator = jnp.einsum("qhd,hde->qhe", query_feat, mem_m, precision=highest)
        denominator = jnp.einsum("qhd,hd->qh", query_feat, mem_z, precision=highest)
        recalled = numerator / jnp.maximum(denominator, 1.0)[..., None]
        gate_value = gate_all[g * group_heads:(g + 1) * group_heads][None, :, None]
        combined = (
            (gate_value * recalled + (1.0 - gate_value) * local_out)
            .astype(bf16)
            .reshape(seg, group_width)
        )

        outgoing = jnp.take(combined, pslot, axis=0, mode="clip").reshape(n, cap, group_width)
        incoming = lax.all_to_all(outgoing, "ctx", 0, 0, tiled=True).reshape(slots, group_width)
        rows = jnp.take(incoming, send_slot, axis=0, mode="clip")
        gathered = lax.all_gather(rows, "head", axis=1, tiled=True)
        return jnp.dot(
            gathered,
            weight_parts[:, g].reshape(head_count * group_width, out_cols),
            preferred_element_type=f32,
        )

    summed = one_group(0)
    for g in range(1, groups):
        summed = summed + one_group(g)
    return summed.astype(bf16)


def solution(mesh):
    return jax.shard_map(
        per_device,
        mesh=mesh,
        in_specs=(
            P("ctx", "head"),
            P("ctx", "head"),
            P("ctx", "head"),
            P(),
            P(),
            P("head"),
            P(None, "head"),
        ),
        out_specs=P("ctx", "head"),
        check_vma=False,
    )
```

```python
import jax
import jax.numpy as jnp
from jax import lax
from jax.sharding import PartitionSpec as P


def feature(inputs):
    return jax.nn.elu(inputs) + 1.0


def per_device(queries, keys, values, row_target, seg_doc, mem_gate, out_weight):
    highest = lax.Precision.HIGHEST
    f32, bf16 = jnp.float32, jnp.bfloat16
    n = lax.axis_size("ctx")
    me = lax.axis_index("ctx")
    seg, width = queries.shape
    heads = mem_gate.shape[0]
    dh = width // heads
    cap = seg // n + (seg // n) // 2
    slots = n * cap

    targets = row_target.reshape(n, seg)
    r_idx = jnp.arange(seg, dtype=jnp.int32)
    o_idx = jnp.arange(n, dtype=jnp.int32)
    s_idx = jnp.arange(slots, dtype=jnp.int32)
    w_idx = jnp.arange(cap, dtype=jnp.int32)
    lower = (r_idx[None, :] < r_idx[:, None]).astype(bf16)

    mine = lax.dynamic_index_in_dim(targets, me, 0, keepdims=False)
    owner = mine // seg
    match = (owner[:, None] == o_idx[None, :]).astype(bf16)
    before = jnp.dot(lower, match, preferred_element_type=f32)
    within = jnp.sum(jnp.where(match > 0, before, 0.0), axis=1).astype(jnp.int32)
    send_slot = owner * cap + within
    slot_row = jnp.sum(
        jnp.where(send_slot[None, :] == s_idx[:, None], r_idx[None, :], 0), axis=1
    )

    arrived = (targets // seg) == me
    rank = jnp.dot(arrived.astype(bf16), lower.T, preferred_element_type=f32).astype(jnp.int32)
    hit = arrived[:, None, :] & (rank[:, None, :] == w_idx[None, :, None])
    pslot = jnp.sum(jnp.where(hit, (targets % seg)[:, None, :], 0), axis=2).reshape(slots)
    count = jnp.sum(arrived.astype(jnp.int32), axis=1)
    valid = (w_idx[None, :] < count[:, None]).reshape(slots)
    tok_slot = jnp.sum(
        jnp.where((pslot[None, :] == r_idx[:, None]) & valid[None, :], s_idx[None, :], 0),
        axis=1,
    )

    doc = seg_doc[me]
    start = jnp.min(jnp.where(seg_doc == doc, o_idx, n))
    score_scale = dh ** (-0.5)
    causal = r_idx[:, None] >= r_idx[None, :]
    head_count = lax.axis_size("head")
    out_cols = out_weight.shape[1]
    bounds = [0, heads - heads // 4, heads]
    weight_rows = out_weight.reshape(head_count, heads, dh, out_cols)
    gate_all = jax.nn.sigmoid(mem_gate)
    shifts = []
    step = 1
    while step < n:
        shifts.append(step)
        step *= 2

    joined = jnp.concatenate([keys, values, queries], axis=1)
    buffer = jnp.take(joined, slot_row, axis=0, mode="clip").reshape(n, cap, 3 * width)
    got = lax.all_to_all(buffer, "ctx", 0, 0, tiled=True).reshape(slots, 3 * width)
    arrived_rows = jnp.take(got, tok_slot, axis=0, mode="clip").reshape(seg, 3, heads, dh)

    def local_attention(query_part, key_part, value_part):
        scores = jnp.einsum(
            "qhd,khd->hqk", query_part, key_part, preferred_element_type=f32
        ) * score_scale
        scores = jnp.where(causal[None], scores, -1e30)
        row_max = jnp.max(scores, axis=-1, keepdims=True)
        weights = jnp.exp(scores - row_max)
        probabilities = (weights / jnp.sum(weights, axis=-1, keepdims=True)).astype(bf16)
        return jnp.einsum(
            "hqk,khd->qhd", probabilities, value_part, preferred_element_type=f32
        )

    def one_group(g, hold):
        first, last = bounds[g], bounds[g + 1]
        group_heads = last - first
        group_width = group_heads * dh
        cuts = [first + round(group_heads * i / len(shifts)) for i in range(len(shifts) + 1)]
        cuts = [c - first for c in cuts]
        key_heads = arrived_rows[:, 0, first:last]
        value_heads = arrived_rows[:, 1, first:last]
        query_heads = arrived_rows[:, 2, first:last]

        key_feat = feature(key_heads.astype(f32))
        delta_m = jnp.einsum(
            "khd,khe->hde", key_feat, value_heads.astype(f32), precision=highest
        )
        delta_z = jnp.sum(key_feat, axis=0)
        delta = jnp.concatenate([delta_m, delta_z[:, None, :]], axis=1)
        if hold is not None:
            delta, _ = lax.optimization_barrier((delta, hold))

        pieces = []
        total = delta
        for k, step in enumerate(shifts):
            lo, hi = cuts[k], cuts[k + 1]
            total, operands = lax.optimization_barrier(
                (total, (query_heads[:, lo:hi], key_heads[:, lo:hi], value_heads[:, lo:hi]))
            )
            perm = [(j, j + step) for j in range(n - step)]
            got = lax.ppermute(total, "ctx", perm)
            if hi > lo:
                piece = local_attention(*operands)
                got, piece = lax.optimization_barrier((got, piece))
                pieces.append(piece)
            total = total + jnp.where(me - step >= start, got, jnp.zeros_like(got))
        local_out = jnp.concatenate(pieces, axis=1)
        memory = total - delta
        mem_m = memory[:, :dh, :]
        mem_z = memory[:, dh, :]

        query_feat = feature(query_heads.astype(f32))
        numerator = jnp.einsum("qhd,hde->qhe", query_feat, mem_m, precision=highest)
        denominator = jnp.einsum("qhd,hd->qh", query_feat, mem_z, precision=highest)
        recalled = numerator / jnp.maximum(denominator, 1.0)[..., None]
        gate_value = gate_all[first:last][None, :, None]
        combined = (
            (gate_value * recalled + (1.0 - gate_value) * local_out)
            .astype(bf16)
            .reshape(seg, group_width)
        )

        outgoing = jnp.take(combined, pslot, axis=0, mode="clip").reshape(n, cap, group_width)
        incoming = lax.all_to_all(outgoing, "ctx", 0, 0, tiled=True).reshape(slots, group_width)
        rows = jnp.take(incoming, send_slot, axis=0, mode="clip")
        gathered = lax.all_gather(rows, "head", axis=1, tiled=True)
        part = jnp.dot(
            gathered,
            weight_rows[:, first:last].reshape(head_count * group_width, out_cols),
            preferred_element_type=f32,
        )
        return part, combined

    summed, hold = one_group(0, None)
    for g in range(1, len(bounds) - 1):
        part, hold = one_group(g, hold)
        summed = summed + part
    return summed.astype(bf16)


def solution(mesh):
    return jax.shard_map(
        per_device,
        mesh=mesh,
        in_specs=(
            P("ctx", "head"),
            P("ctx", "head"),
            P("ctx", "head"),
            P(),
            P(),
            P("head"),
            P(None, "head"),
        ),
        out_specs=P("ctx", "head"),
        check_vma=False,
    )
```

```python
import jax
import jax.numpy as jnp
from jax import lax
from jax.sharding import PartitionSpec as P


def feature(inputs):
    return jax.nn.elu(inputs) + 1.0


def per_device(queries, keys, values, row_target, seg_doc, mem_gate, out_weight):
    highest = lax.Precision.HIGHEST
    f32, bf16 = jnp.float32, jnp.bfloat16
    n = lax.axis_size("ctx")
    me = lax.axis_index("ctx")
    seg, width = queries.shape
    heads = mem_gate.shape[0]
    dh = width // heads
    cap = seg // n + (seg // n) // 2
    slots = n * cap

    targets = row_target.reshape(n, seg)
    r_idx = jnp.arange(seg, dtype=jnp.int32)
    o_idx = jnp.arange(n, dtype=jnp.int32)
    s_idx = jnp.arange(slots, dtype=jnp.int32)
    w_idx = jnp.arange(cap, dtype=jnp.int32)
    lower = (r_idx[None, :] < r_idx[:, None]).astype(bf16)

    mine = lax.dynamic_index_in_dim(targets, me, 0, keepdims=False)
    owner = mine // seg
    match = (owner[:, None] == o_idx[None, :]).astype(bf16)
    before = jnp.dot(lower, match, preferred_element_type=f32)
    within = jnp.sum(jnp.where(match > 0, before, 0.0), axis=1).astype(jnp.int32)
    send_slot = owner * cap + within
    slot_row = jnp.sum(
        jnp.where(send_slot[None, :] == s_idx[:, None], r_idx[None, :], 0), axis=1
    )

    arrived = (targets // seg) == me
    rank = jnp.dot(arrived.astype(bf16), lower.T, preferred_element_type=f32).astype(jnp.int32)
    hit = arrived[:, None, :] & (rank[:, None, :] == w_idx[None, :, None])
    pslot = jnp.sum(jnp.where(hit, (targets % seg)[:, None, :], 0), axis=2).reshape(slots)
    count = jnp.sum(arrived.astype(jnp.int32), axis=1)
    valid = (w_idx[None, :] < count[:, None]).reshape(slots)
    tok_slot = jnp.sum(
        jnp.where((pslot[None, :] == r_idx[:, None]) & valid[None, :], s_idx[None, :], 0),
        axis=1,
    )

    doc = seg_doc[me]
    start = jnp.min(jnp.where(seg_doc == doc, o_idx, n))
    score_scale = dh ** (-0.5)
    causal = r_idx[:, None] >= r_idx[None, :]
    head_count = lax.axis_size("head")
    out_cols = out_weight.shape[1]
    bounds = [0, heads // 2, heads]
    weight_rows = out_weight.reshape(head_count, heads, dh, out_cols)
    gate_all = jax.nn.sigmoid(mem_gate)
    shifts = []
    step = 1
    while step < n:
        shifts.append(step)
        step *= 2

    def dispatch(source):
        buffer = jnp.take(source, slot_row, axis=0, mode="clip").reshape(n, cap, width)
        got = lax.all_to_all(buffer, "ctx", 0, 0, tiled=True).reshape(slots, width)
        return jnp.take(got, tok_slot, axis=0, mode="clip").reshape(seg, heads, dh)

    key_all = dispatch(keys)
    value_all = dispatch(values)
    query_all = dispatch(queries)

    def local_attention(query_part, key_part, value_part):
        scores = jnp.einsum(
            "qhd,khd->hqk", query_part, key_part, preferred_element_type=f32
        ) * score_scale
        scores = jnp.where(causal[None], scores, -1e30)
        row_max = jnp.max(scores, axis=-1, keepdims=True)
        weights = jnp.exp(scores - row_max)
        probabilities = (weights / jnp.sum(weights, axis=-1, keepdims=True)).astype(bf16)
        return jnp.einsum(
            "hqk,khd->qhd", probabilities, value_part, preferred_element_type=f32
        )

    def one_group(g, hold):
        first, last = bounds[g], bounds[g + 1]
        group_heads = last - first
        group_width = group_heads * dh
        cuts = [first + round(group_heads * i / len(shifts)) for i in range(len(shifts) + 1)]
        cuts = [c - first for c in cuts]
        key_heads = key_all[:, first:last]
        value_heads = value_all[:, first:last]
        query_heads = query_all[:, first:last]

        key_feat = feature(key_heads.astype(f32))
        delta_m = jnp.einsum(
            "khd,khe->hde", key_feat, value_heads.astype(f32), precision=highest
        )
        delta_z = jnp.sum(key_feat, axis=0)
        delta = jnp.concatenate([delta_m, delta_z[:, None, :]], axis=1)
        if hold is not None:
            delta, _ = lax.optimization_barrier((delta, hold))

        pieces = []
        total = delta
        for k, step in enumerate(shifts):
            lo, hi = cuts[k], cuts[k + 1]
            total, operands = lax.optimization_barrier(
                (total, (query_heads[:, lo:hi], key_heads[:, lo:hi], value_heads[:, lo:hi]))
            )
            perm = [(j, j + step) for j in range(n - step)]
            got = lax.ppermute(total, "ctx", perm)
            if hi > lo:
                piece = local_attention(*operands)
                got, piece = lax.optimization_barrier((got, piece))
                pieces.append(piece)
            total = total + jnp.where(me - step >= start, got, jnp.zeros_like(got))
        local_out = jnp.concatenate(pieces, axis=1)
        memory = total - delta
        mem_m = memory[:, :dh, :]
        mem_z = memory[:, dh, :]

        query_feat = feature(query_heads.astype(f32))
        numerator = jnp.einsum("qhd,hde->qhe", query_feat, mem_m, precision=highest)
        denominator = jnp.einsum("qhd,hd->qh", query_feat, mem_z, precision=highest)
        recalled = numerator / jnp.maximum(denominator, 1.0)[..., None]
        gate_value = gate_all[first:last][None, :, None]
        combined = (
            (gate_value * recalled + (1.0 - gate_value) * local_out)
            .astype(bf16)
            .reshape(seg, group_width)
        )

        outgoing = jnp.take(combined, pslot, axis=0, mode="clip").reshape(n, cap, group_width)
        incoming = lax.all_to_all(outgoing, "ctx", 0, 0, tiled=True).reshape(slots, group_width)
        rows = jnp.take(incoming, send_slot, axis=0, mode="clip")
        gathered = lax.all_gather(rows, "head", axis=1, tiled=True)
        part = jnp.dot(
            gathered,
            weight_rows[:, first:last].reshape(head_count * group_width, out_cols),
            preferred_element_type=f32,
        )
        return part, combined

    summed, hold = one_group(0, None)
    for g in range(1, len(bounds) - 1):
        part, hold = one_group(g, hold)
        summed = summed + part
    return summed.astype(bf16)


def solution(mesh):
    return jax.shard_map(
        per_device,
        mesh=mesh,
        in_specs=(
            P("ctx", "head"),
            P("ctx", "head"),
            P("ctx", "head"),
            P(),
            P(),
            P("head"),
            P(None, "head"),
        ),
        out_specs=P("ctx", "head"),
        check_vma=False,
    )
```

```python
import jax
import jax.numpy as jnp
from jax import lax
from jax.sharding import PartitionSpec as P


def feature(inputs):
    return jax.nn.elu(inputs) + 1.0


def per_device(queries, keys, values, row_target, seg_doc, mem_gate, out_weight):
    highest = lax.Precision.HIGHEST
    f32, bf16 = jnp.float32, jnp.bfloat16
    n = lax.axis_size("ctx")
    me = lax.axis_index("ctx")
    seg, width = queries.shape
    heads = mem_gate.shape[0]
    dh = width // heads
    cap = seg // n + (seg // n) // 2
    slots = n * cap

    targets = row_target.reshape(n, seg)
    r_idx = jnp.arange(seg, dtype=jnp.int32)
    o_idx = jnp.arange(n, dtype=jnp.int32)
    s_idx = jnp.arange(slots, dtype=jnp.int32)
    w_idx = jnp.arange(cap, dtype=jnp.int32)
    lower = (r_idx[None, :] < r_idx[:, None]).astype(bf16)

    mine = lax.dynamic_index_in_dim(targets, me, 0, keepdims=False)
    owner = mine // seg
    match = (owner[:, None] == o_idx[None, :]).astype(bf16)
    before = jnp.dot(lower, match, preferred_element_type=f32)
    within = jnp.sum(jnp.where(match > 0, before, 0.0), axis=1).astype(jnp.int32)
    send_slot = owner * cap + within
    slot_row = jnp.sum(
        jnp.where(send_slot[None, :] == s_idx[:, None], r_idx[None, :], 0), axis=1
    )

    arrived = (targets // seg) == me
    rank = jnp.dot(arrived.astype(bf16), lower.T, preferred_element_type=f32).astype(jnp.int32)
    hit = arrived[:, None, :] & (rank[:, None, :] == w_idx[None, :, None])
    pslot = jnp.sum(jnp.where(hit, (targets % seg)[:, None, :], 0), axis=2).reshape(slots)
    count = jnp.sum(arrived.astype(jnp.int32), axis=1)
    valid = (w_idx[None, :] < count[:, None]).reshape(slots)
    tok_slot = jnp.sum(
        jnp.where((pslot[None, :] == r_idx[:, None]) & valid[None, :], s_idx[None, :], 0),
        axis=1,
    )

    doc = seg_doc[me]
    start = jnp.min(jnp.where(seg_doc == doc, o_idx, n))
    score_scale = dh ** (-0.5)
    causal = r_idx[:, None] >= r_idx[None, :]
    head_count = lax.axis_size("head")
    out_cols = out_weight.shape[1]
    bounds = [0, heads // 2, heads]
    weight_blocks = out_weight.reshape(head_count, width, out_cols)
    gate_all = jax.nn.sigmoid(mem_gate)
    shifts = []
    step = 1
    while step < n:
        shifts.append(step)
        step *= 2

    def dispatch(source):
        buffer = jnp.take(source, slot_row, axis=0, mode="clip").reshape(n, cap, width)
        got = lax.all_to_all(buffer, "ctx", 0, 0, tiled=True).reshape(slots, width)
        return jnp.take(got, tok_slot, axis=0, mode="clip").reshape(seg, heads, dh)

    key_all = dispatch(keys)
    value_all = dispatch(values)
    query_all = dispatch(queries)

    def local_attention(query_part, key_part, value_part):
        scores = jnp.einsum(
            "qhd,khd->hqk", query_part, key_part, preferred_element_type=f32
        ) * score_scale
        scores = jnp.where(causal[None], scores, -1e30)
        row_max = jnp.max(scores, axis=-1, keepdims=True)
        weights = jnp.exp(scores - row_max)
        probabilities = (weights / jnp.sum(weights, axis=-1, keepdims=True)).astype(bf16)
        return jnp.einsum(
            "hqk,khd->qhd", probabilities, value_part, preferred_element_type=f32
        )

    def one_group(g, hold):
        first, last = bounds[g], bounds[g + 1]
        group_heads = last - first
        group_width = group_heads * dh
        cuts = [first + round(group_heads * i / len(shifts)) for i in range(len(shifts) + 1)]
        cuts = [c - first for c in cuts]
        key_heads = key_all[:, first:last]
        value_heads = value_all[:, first:last]
        query_heads = query_all[:, first:last]

        key_feat = feature(key_heads.astype(f32))
        delta_m = jnp.einsum(
            "khd,khe->hde", key_feat, value_heads.astype(f32), precision=highest
        )
        delta_z = jnp.sum(key_feat, axis=0)
        delta = jnp.concatenate([delta_m, delta_z[:, None, :]], axis=1)
        if hold is not None:
            delta, _ = lax.optimization_barrier((delta, hold))

        pieces = []
        total = delta
        for k, step in enumerate(shifts):
            lo, hi = cuts[k], cuts[k + 1]
            total, operands = lax.optimization_barrier(
                (total, (query_heads[:, lo:hi], key_heads[:, lo:hi], value_heads[:, lo:hi]))
            )
            perm = [(j, j + step) for j in range(n - step)]
            got = lax.ppermute(total, "ctx", perm)
            if hi > lo:
                piece = local_attention(*operands)
                got, piece = lax.optimization_barrier((got, piece))
                pieces.append(piece)
            total = total + jnp.where(me - step >= start, got, jnp.zeros_like(got))
        local_out = jnp.concatenate(pieces, axis=1)
        memory = total - delta
        mem_m = memory[:, :dh, :]
        mem_z = memory[:, dh, :]

        query_feat = feature(query_heads.astype(f32))
        numerator = jnp.einsum("qhd,hde->qhe", query_feat, mem_m, precision=highest)
        denominator = jnp.einsum("qhd,hd->qh", query_feat, mem_z, precision=highest)
        recalled = numerator / jnp.maximum(denominator, 1.0)[..., None]
        gate_value = gate_all[first:last][None, :, None]
        combined = (
            (gate_value * recalled + (1.0 - gate_value) * local_out)
            .astype(bf16)
            .reshape(seg, group_width)
        )

        outgoing = jnp.take(combined, pslot, axis=0, mode="clip").reshape(n, cap, group_width)
        incoming = lax.all_to_all(outgoing, "ctx", 0, 0, tiled=True).reshape(slots, group_width)
        rows = jnp.take(incoming, send_slot, axis=0, mode="clip")
        head_index = lax.axis_index("head")

        def project(block, source):
            weight = lax.dynamic_index_in_dim(weight_blocks, source, 0, keepdims=False)
            return jnp.dot(
                block, weight[first * dh:last * dh], preferred_element_type=f32
            )

        part = project(rows, head_index)
        for shift in range(1, head_count):
            perm = [(j, (j + shift) % head_count) for j in range(head_count)]
            arrived = lax.ppermute(rows, "head", perm)
            part = part + project(arrived, (head_index + head_count - shift) % head_count)
        return part, combined

    summed, hold = one_group(0, None)
    for g in range(1, len(bounds) - 1):
        part, hold = one_group(g, hold)
        summed = summed + part
    return summed.astype(bf16)


def solution(mesh):
    return jax.shard_map(
        per_device,
        mesh=mesh,
        in_specs=(
            P("ctx", "head"),
            P("ctx", "head"),
            P("ctx", "head"),
            P(),
            P(),
            P("head"),
            P(None, "head"),
        ),
        out_specs=P("ctx", "head"),
        check_vma=False,
    )
```

```python
import jax
import jax.numpy as jnp
from jax import lax
from jax.sharding import PartitionSpec as P


def feature(inputs):
    return jax.nn.elu(inputs) + 1.0


def per_device(queries, keys, values, row_target, seg_doc, mem_gate, out_weight):
    highest = lax.Precision.HIGHEST
    f32, bf16 = jnp.float32, jnp.bfloat16
    n = lax.axis_size("ctx")
    me = lax.axis_index("ctx")
    seg, width = queries.shape
    heads = mem_gate.shape[0]
    dh = width // heads
    cap = seg // n + (seg // n) // 2
    slots = n * cap

    targets = row_target.reshape(n, seg)
    r_idx = jnp.arange(seg, dtype=jnp.int32)
    o_idx = jnp.arange(n, dtype=jnp.int32)
    s_idx = jnp.arange(slots, dtype=jnp.int32)
    w_idx = jnp.arange(cap, dtype=jnp.int32)
    lower = (r_idx[None, :] < r_idx[:, None]).astype(bf16)

    mine = lax.dynamic_index_in_dim(targets, me, 0, keepdims=False)
    owner = mine // seg
    match = (owner[:, None] == o_idx[None, :]).astype(bf16)
    before = jnp.dot(lower, match, preferred_element_type=f32)
    within = jnp.sum(jnp.where(match > 0, before, 0.0), axis=1).astype(jnp.int32)
    send_slot = owner * cap + within
    slot_row = jnp.sum(
        jnp.where(send_slot[None, :] == s_idx[:, None], r_idx[None, :], 0), axis=1
    )

    arrived = (targets // seg) == me
    rank = jnp.dot(arrived.astype(bf16), lower.T, preferred_element_type=f32).astype(jnp.int32)
    hit = arrived[:, None, :] & (rank[:, None, :] == w_idx[None, :, None])
    pslot = jnp.sum(jnp.where(hit, (targets % seg)[:, None, :], 0), axis=2).reshape(slots)
    count = jnp.sum(arrived.astype(jnp.int32), axis=1)
    valid = (w_idx[None, :] < count[:, None]).reshape(slots)
    tok_slot = jnp.sum(
        jnp.where((pslot[None, :] == r_idx[:, None]) & valid[None, :], s_idx[None, :], 0),
        axis=1,
    )

    doc = seg_doc[me]
    start = jnp.min(jnp.where(seg_doc == doc, o_idx, n))
    score_scale = dh ** (-0.5)
    causal = r_idx[:, None] >= r_idx[None, :]
    head_count = lax.axis_size("head")
    out_cols = out_weight.shape[1]
    bounds = [0, heads // 2, heads]
    weight_rows = out_weight.reshape(head_count, heads, dh, out_cols)
    gate_all = jax.nn.sigmoid(mem_gate)
    rounds = []
    base = 1
    while base < n:
        rounds.append([k * base for k in range(1, 4) if k * base < n])
        base *= 4

    def dispatch(source):
        buffer = jnp.take(source, slot_row, axis=0, mode="clip").reshape(n, cap, width)
        got = lax.all_to_all(buffer, "ctx", 0, 0, tiled=True).reshape(slots, width)
        return jnp.take(got, tok_slot, axis=0, mode="clip").reshape(seg, heads, dh)

    key_all = dispatch(keys)
    weight_parts = [
        weight_rows[:, bounds[g]:bounds[g + 1]].reshape(head_count * (bounds[g + 1] - bounds[g]) * dh, out_cols)
        for g in range(len(bounds) - 1)
    ]
    key_all, weight_parts = lax.optimization_barrier((key_all, weight_parts))
    value_all = dispatch(values)
    query_all = dispatch(queries)

    def local_attention(query_part, key_part, value_part):
        scores = jnp.einsum(
            "qhd,khd->hqk", query_part, key_part, preferred_element_type=f32
        ) * score_scale
        scores = jnp.where(causal[None], scores, -1e30)
        row_max = jnp.max(scores, axis=-1, keepdims=True)
        weights = jnp.exp(scores - row_max)
        probabilities = (weights / jnp.sum(weights, axis=-1, keepdims=True)).astype(bf16)
        return jnp.einsum(
            "hqk,khd->qhd", probabilities, value_part, preferred_element_type=f32
        )

    def one_group(g, hold):
        first, last = bounds[g], bounds[g + 1]
        group_heads = last - first
        group_width = group_heads * dh
        cuts = [first + round(group_heads * i / len(rounds)) for i in range(len(rounds) + 1)]
        cuts = [c - first for c in cuts]
        key_heads = key_all[:, first:last]
        value_heads = value_all[:, first:last]
        query_heads = query_all[:, first:last]

        key_feat = feature(key_heads.astype(f32))
        delta_m = jnp.einsum(
            "khd,khe->hde", key_feat, value_heads.astype(f32), precision=highest
        )
        delta_z = jnp.sum(key_feat, axis=0)
        delta = jnp.concatenate([delta_m, delta_z[:, None, :]], axis=1)
        if hold is not None:
            delta, _ = lax.optimization_barrier((delta, hold))

        pieces = []
        total = delta
        for k, shifts in enumerate(rounds):
            lo, hi = cuts[k], cuts[k + 1]
            total, operands = lax.optimization_barrier(
                (total, (query_heads[:, lo:hi], key_heads[:, lo:hi], value_heads[:, lo:hi]))
            )
            arrivals = [
                lax.ppermute(total, "ctx", [(j, j + shift) for j in range(n - shift)])
                for shift in shifts
            ]
            if hi > lo:
                piece = local_attention(*operands)
                arrivals, piece = lax.optimization_barrier((arrivals, piece))
                pieces.append(piece)
            for shift, got in zip(shifts, arrivals):
                total = total + jnp.where(me - shift >= start, got, jnp.zeros_like(got))
        local_out = jnp.concatenate(pieces, axis=1)
        memory = total - delta
        mem_m = memory[:, :dh, :]
        mem_z = memory[:, dh, :]

        query_feat = feature(query_heads.astype(f32))
        numerator = jnp.einsum("qhd,hde->qhe", query_feat, mem_m, precision=highest)
        denominator = jnp.einsum("qhd,hd->qh", query_feat, mem_z, precision=highest)
        recalled = numerator / jnp.maximum(denominator, 1.0)[..., None]
        gate_value = gate_all[first:last][None, :, None]
        combined = (
            (gate_value * recalled + (1.0 - gate_value) * local_out)
            .astype(bf16)
            .reshape(seg, group_width)
        )

        outgoing = jnp.take(combined, pslot, axis=0, mode="clip").reshape(n, cap, group_width)
        incoming = lax.all_to_all(outgoing, "ctx", 0, 0, tiled=True).reshape(slots, group_width)
        rows = jnp.take(incoming, send_slot, axis=0, mode="clip")
        gathered = lax.all_gather(rows, "head", axis=1, tiled=True)
        part = jnp.dot(
            gathered,
            weight_parts[g],
            preferred_element_type=f32,
        )
        return part, combined

    summed, hold = one_group(0, None)
    for g in range(1, len(bounds) - 1):
        part, hold = one_group(g, hold)
        summed = summed + part
    return summed.astype(bf16)


def solution(mesh):
    return jax.shard_map(
        per_device,
        mesh=mesh,
        in_specs=(
            P("ctx", "head"),
            P("ctx", "head"),
            P("ctx", "head"),
            P(),
            P(),
            P("head"),
            P(None, "head"),
        ),
        out_specs=P("ctx", "head"),
        check_vma=False,
    )
```

```python
import jax
import jax.numpy as jnp
from jax import lax
from jax.sharding import PartitionSpec as P


def feature(inputs):
    return jax.nn.elu(inputs) + 1.0


def per_device(queries, keys, values, row_target, seg_doc, mem_gate, out_weight):
    highest = lax.Precision.HIGHEST
    f32, bf16 = jnp.float32, jnp.bfloat16
    n = lax.axis_size("ctx")
    me = lax.axis_index("ctx")
    seg, width = queries.shape
    heads = mem_gate.shape[0]
    dh = width // heads
    cap = seg // n + (seg // n) // 2
    slots = n * cap

    targets = row_target.reshape(n, seg)
    r_idx = jnp.arange(seg, dtype=jnp.int32)
    o_idx = jnp.arange(n, dtype=jnp.int32)
    s_idx = jnp.arange(slots, dtype=jnp.int32)
    w_idx = jnp.arange(cap, dtype=jnp.int32)
    lower = (r_idx[None, :] < r_idx[:, None]).astype(bf16)

    mine = lax.dynamic_index_in_dim(targets, me, 0, keepdims=False)
    owner = mine // seg
    match = (owner[:, None] == o_idx[None, :]).astype(bf16)
    before = jnp.dot(lower, match, preferred_element_type=f32)
    within = jnp.sum(jnp.where(match > 0, before, 0.0), axis=1).astype(jnp.int32)
    send_slot = owner * cap + within
    slot_row = jnp.sum(
        jnp.where(send_slot[None, :] == s_idx[:, None], r_idx[None, :], 0), axis=1
    )

    arrived = (targets // seg) == me
    rank = jnp.dot(arrived.astype(bf16), lower.T, preferred_element_type=f32).astype(jnp.int32)
    hit = arrived[:, None, :] & (rank[:, None, :] == w_idx[None, :, None])
    pslot = jnp.sum(jnp.where(hit, (targets % seg)[:, None, :], 0), axis=2).reshape(slots)
    count = jnp.sum(arrived.astype(jnp.int32), axis=1)
    valid = (w_idx[None, :] < count[:, None]).reshape(slots)
    tok_slot = jnp.sum(
        jnp.where((pslot[None, :] == r_idx[:, None]) & valid[None, :], s_idx[None, :], 0),
        axis=1,
    )

    doc = seg_doc[me]
    start = jnp.min(jnp.where(seg_doc == doc, o_idx, n))
    score_scale = dh ** (-0.5)
    causal = r_idx[:, None] >= r_idx[None, :]
    head_count = lax.axis_size("head")
    out_cols = out_weight.shape[1]
    bounds = [0, heads - (3 * heads) // 8, heads]
    weight_rows = out_weight.reshape(head_count, heads, dh, out_cols)
    gate_all = jax.nn.sigmoid(mem_gate)
    shifts = []
    step = 1
    while step < n:
        shifts.append(step)
        step *= 2

    def dispatch(source):
        buffer = jnp.take(source, slot_row, axis=0, mode="clip").reshape(n, cap, width)
        got = lax.all_to_all(buffer, "ctx", 0, 0, tiled=True).reshape(slots, width)
        return jnp.take(got, tok_slot, axis=0, mode="clip").reshape(seg, heads, dh)

    key_all = dispatch(keys)
    weight_parts = [
        weight_rows[:, bounds[g]:bounds[g + 1]].reshape(
            head_count * (bounds[g + 1] - bounds[g]) * dh, out_cols
        )
        for g in range(len(bounds) - 1)
    ]
    value_all = dispatch(values)
    query_all = dispatch(queries)

    def local_attention(query_part, key_part, value_part):
        scores = jnp.einsum(
            "qhd,khd->hqk", query_part, key_part, preferred_element_type=f32
        ) * score_scale
        scores = jnp.where(causal[None], scores, -1e30)
        row_max = jnp.max(scores, axis=-1, keepdims=True)
        weights = jnp.exp(scores - row_max)
        probabilities = (weights / jnp.sum(weights, axis=-1, keepdims=True)).astype(bf16)
        return jnp.einsum(
            "hqk,khd->qhd", probabilities, value_part, preferred_element_type=f32
        )

    def one_group(g, hold, weights):
        first, last = bounds[g], bounds[g + 1]
        group_heads = last - first
        group_width = group_heads * dh
        cuts = [first + round(group_heads * i / len(shifts)) for i in range(len(shifts) + 1)]
        cuts = [c - first for c in cuts]
        key_heads = key_all[:, first:last]
        value_heads = value_all[:, first:last]
        query_heads = query_all[:, first:last]

        key_feat = feature(key_heads.astype(f32))
        delta_m = jnp.einsum(
            "khd,khe->hde", key_feat, value_heads.astype(f32), precision=highest
        )
        delta_z = jnp.sum(key_feat, axis=0)
        delta = jnp.concatenate([delta_m, delta_z[:, None, :]], axis=1)
        if hold is not None:
            delta, _ = lax.optimization_barrier((delta, hold[0]))

        pieces = []
        total = delta
        for k, step in enumerate(shifts):
            lo, hi = cuts[k], cuts[k + 1]
            total, operands = lax.optimization_barrier(
                (total, (query_heads[:, lo:hi], key_heads[:, lo:hi], value_heads[:, lo:hi]))
            )
            if hold is not None and k == 1:
                total, _ = lax.optimization_barrier((total, hold[1]))
            perm = [(j, j + step) for j in range(n - step)]
            got = lax.ppermute(total, "ctx", perm)
            if hi > lo:
                piece = local_attention(*operands)
                got, piece = lax.optimization_barrier((got, piece))
                pieces.append(piece)
            total = total + jnp.where(me - step >= start, got, jnp.zeros_like(got))
        local_out = jnp.concatenate(pieces, axis=1)
        memory = total - delta
        mem_m = memory[:, :dh, :]
        mem_z = memory[:, dh, :]

        query_feat = feature(query_heads.astype(f32))
        numerator = jnp.einsum("qhd,hde->qhe", query_feat, mem_m, precision=highest)
        denominator = jnp.einsum("qhd,hd->qh", query_feat, mem_z, precision=highest)
        recalled = numerator / jnp.maximum(denominator, 1.0)[..., None]
        gate_value = gate_all[first:last][None, :, None]
        combined = (
            (gate_value * recalled + (1.0 - gate_value) * local_out)
            .astype(bf16)
            .reshape(seg, group_width)
        )

        outgoing = jnp.take(combined, pslot, axis=0, mode="clip").reshape(n, cap, group_width)
        incoming = lax.all_to_all(outgoing, "ctx", 0, 0, tiled=True).reshape(slots, group_width)
        rows = jnp.take(incoming, send_slot, axis=0, mode="clip")
        gathered = lax.all_gather(rows, "head", axis=1, tiled=True)
        part = jnp.dot(
            gathered,
            weights[g],
            preferred_element_type=f32,
        )
        return part, (combined, rows), weights

    summed, hold, weight_parts = one_group(0, None, weight_parts)
    for g in range(1, len(bounds) - 1):
        part, hold, weight_parts = one_group(g, hold, weight_parts)
        summed = summed + part
    return summed.astype(bf16)


def solution(mesh):
    return jax.shard_map(
        per_device,
        mesh=mesh,
        in_specs=(
            P("ctx", "head"),
            P("ctx", "head"),
            P("ctx", "head"),
            P(),
            P(),
            P("head"),
            P(None, "head"),
        ),
        out_specs=P("ctx", "head"),
        check_vma=False,
    )
```

```python
import jax
import jax.numpy as jnp
from jax import lax
from jax.sharding import PartitionSpec as P


def feature(inputs):
    return jax.nn.elu(inputs) + 1.0


def per_device(queries, keys, values, row_target, seg_doc, mem_gate, out_weight):
    highest = lax.Precision.HIGHEST
    f32, bf16 = jnp.float32, jnp.bfloat16
    n = lax.axis_size("ctx")
    me = lax.axis_index("ctx")
    seg, width = queries.shape
    heads = mem_gate.shape[0]
    dh = width // heads
    cap = seg // n + (seg // n) // 2
    slots = n * cap

    targets = row_target.reshape(n, seg)
    r_idx = jnp.arange(seg, dtype=jnp.int32)
    o_idx = jnp.arange(n, dtype=jnp.int32)
    s_idx = jnp.arange(slots, dtype=jnp.int32)
    w_idx = jnp.arange(cap, dtype=jnp.int32)
    lower = (r_idx[None, :] < r_idx[:, None]).astype(bf16)

    mine = lax.dynamic_index_in_dim(targets, me, 0, keepdims=False)
    owner = mine // seg
    match = (owner[:, None] == o_idx[None, :]).astype(bf16)
    before = jnp.dot(lower, match, preferred_element_type=f32)
    within = jnp.sum(jnp.where(match > 0, before, 0.0), axis=1).astype(jnp.int32)
    send_slot = owner * cap + within
    slot_row = jnp.sum(
        jnp.where(send_slot[None, :] == s_idx[:, None], r_idx[None, :], 0), axis=1
    )

    arrived = (targets // seg) == me
    rank = jnp.dot(arrived.astype(bf16), lower.T, preferred_element_type=f32).astype(jnp.int32)
    hit = arrived[:, None, :] & (rank[:, None, :] == w_idx[None, :, None])
    pslot = jnp.sum(jnp.where(hit, (targets % seg)[:, None, :], 0), axis=2).reshape(slots)
    count = jnp.sum(arrived.astype(jnp.int32), axis=1)
    valid = (w_idx[None, :] < count[:, None]).reshape(slots)
    tok_slot = jnp.sum(
        jnp.where((pslot[None, :] == r_idx[:, None]) & valid[None, :], s_idx[None, :], 0),
        axis=1,
    )

    doc = seg_doc[me]
    start = jnp.min(jnp.where(seg_doc == doc, o_idx, n))
    score_scale = dh ** (-0.5)
    causal = r_idx[:, None] >= r_idx[None, :]
    head_count = lax.axis_size("head")
    out_cols = out_weight.shape[1]
    bounds = [0, heads - heads // 4, heads]
    weight_rows = out_weight.reshape(head_count, heads, dh, out_cols)
    gate_all = jax.nn.sigmoid(mem_gate)
    shifts = []
    step = 1
    while step < n:
        shifts.append(step)
        step *= 2

    def dispatch(source):
        buffer = jnp.take(source, slot_row, axis=0, mode="clip").reshape(n, cap, width)
        got = lax.all_to_all(buffer, "ctx", 0, 0, tiled=True).reshape(slots, width)
        return jnp.take(got, tok_slot, axis=0, mode="clip").reshape(seg, heads, dh)

    key_all = dispatch(keys)
    weight_parts = [
        weight_rows[:, bounds[g]:bounds[g + 1]].reshape(
            head_count * (bounds[g + 1] - bounds[g]) * dh, out_cols
        )
        for g in range(len(bounds) - 1)
    ]
    value_all = dispatch(values)
    query_all = dispatch(queries)

    def local_attention(query_part, key_part, value_part):
        scores = jnp.einsum(
            "qhd,khd->hqk", query_part, key_part, preferred_element_type=f32
        ) * score_scale
        scores = jnp.where(causal[None], scores, -1e30)
        row_max = jnp.max(scores, axis=-1, keepdims=True)
        weights = jnp.exp(scores - row_max)
        probabilities = (weights / jnp.sum(weights, axis=-1, keepdims=True)).astype(bf16)
        return jnp.einsum(
            "hqk,khd->qhd", probabilities, value_part, preferred_element_type=f32
        )

    def one_group(g, hold, weights):
        first, last = bounds[g], bounds[g + 1]
        group_heads = last - first
        group_width = group_heads * dh
        cuts = [first + round(group_heads * i / len(shifts)) for i in range(len(shifts) + 1)]
        cuts = [c - first for c in cuts]
        key_heads = key_all[:, first:last]
        value_heads = value_all[:, first:last]
        query_heads = query_all[:, first:last]

        key_feat = feature(key_heads.astype(f32))
        delta_m = jnp.einsum(
            "khd,khe->hde", key_feat, value_heads.astype(f32), precision=highest
        )
        delta_z = jnp.sum(key_feat, axis=0)
        delta = jnp.concatenate([delta_m, delta_z[:, None, :]], axis=1)
        if hold is not None:
            delta, _ = lax.optimization_barrier((delta, hold[0]))

        pieces = []
        total = delta
        for k, step in enumerate(shifts):
            lo, hi = cuts[k], cuts[k + 1]
            total, operands = lax.optimization_barrier(
                (total, (query_heads[:, lo:hi], key_heads[:, lo:hi], value_heads[:, lo:hi]))
            )
            if hold is not None and k == 1:
                total, _ = lax.optimization_barrier((total, hold[1]))
            perm = [(j, j + step) for j in range(n - step)]
            got = lax.ppermute(total, "ctx", perm)
            if hi > lo:
                piece = local_attention(*operands)
                got, piece = lax.optimization_barrier((got, piece))
                pieces.append(piece)
            total = total + jnp.where(me - step >= start, got, jnp.zeros_like(got))
        local_out = jnp.concatenate(pieces, axis=1)
        memory = total - delta
        mem_m = memory[:, :dh, :]
        mem_z = memory[:, dh, :]

        query_feat = feature(query_heads.astype(f32))
        numerator = jnp.einsum("qhd,hde->qhe", query_feat, mem_m, precision=highest)
        denominator = jnp.einsum("qhd,hd->qh", query_feat, mem_z, precision=highest)
        recalled = numerator / jnp.maximum(denominator, 1.0)[..., None]
        gate_value = gate_all[first:last][None, :, None]
        combined = (
            (gate_value * recalled + (1.0 - gate_value) * local_out)
            .astype(bf16)
            .reshape(seg, group_width)
        )

        outgoing = jnp.take(combined, pslot, axis=0, mode="clip").reshape(n, cap, group_width)
        incoming = lax.all_to_all(outgoing, "ctx", 0, 0, tiled=True).reshape(slots, group_width)
        rows = jnp.take(incoming, send_slot, axis=0, mode="clip")
        gathered = lax.all_gather(rows, "head", axis=1, tiled=True)
        part = jnp.dot(
            gathered,
            weights[g],
            preferred_element_type=f32,
        )
        return part, (combined, rows), weights

    summed, hold, weight_parts = one_group(0, None, weight_parts)
    for g in range(1, len(bounds) - 1):
        part, hold, weight_parts = one_group(g, hold, weight_parts)
        summed = summed + part
    return summed.astype(bf16)


def solution(mesh):
    return jax.shard_map(
        per_device,
        mesh=mesh,
        in_specs=(
            P("ctx", "head"),
            P("ctx", "head"),
            P("ctx", "head"),
            P(),
            P(),
            P("head"),
            P(None, "head"),
        ),
        out_specs=P("ctx", "head"),
        check_vma=False,
    )
```

```python
import jax
import jax.numpy as jnp
from jax import lax
from jax.sharding import PartitionSpec as P


def feature(inputs):
    return jax.nn.elu(inputs) + 1.0


def per_device(queries, keys, values, row_target, seg_doc, mem_gate, out_weight):
    highest = lax.Precision.HIGHEST
    f32, bf16 = jnp.float32, jnp.bfloat16
    n = lax.axis_size("ctx")
    me = lax.axis_index("ctx")
    seg, width = queries.shape
    heads = mem_gate.shape[0]
    dh = width // heads
    cap = seg // n + (seg // n) // 2
    slots = n * cap

    targets = row_target.reshape(n, seg)
    r_idx = jnp.arange(seg, dtype=jnp.int32)
    o_idx = jnp.arange(n, dtype=jnp.int32)
    s_idx = jnp.arange(slots, dtype=jnp.int32)
    w_idx = jnp.arange(cap, dtype=jnp.int32)
    lower = (r_idx[None, :] < r_idx[:, None]).astype(bf16)

    mine = lax.dynamic_index_in_dim(targets, me, 0, keepdims=False)
    owner = mine // seg
    match = (owner[:, None] == o_idx[None, :]).astype(bf16)
    before = jnp.dot(lower, match, preferred_element_type=f32)
    within = jnp.sum(jnp.where(match > 0, before, 0.0), axis=1).astype(jnp.int32)
    send_slot = owner * cap + within
    slot_row = jnp.sum(
        jnp.where(send_slot[None, :] == s_idx[:, None], r_idx[None, :], 0), axis=1
    )

    arrived = (targets // seg) == me
    rank = jnp.dot(arrived.astype(bf16), lower.T, preferred_element_type=f32).astype(jnp.int32)
    hit = arrived[:, None, :] & (rank[:, None, :] == w_idx[None, :, None])
    pslot = jnp.sum(jnp.where(hit, (targets % seg)[:, None, :], 0), axis=2).reshape(slots)
    count = jnp.sum(arrived.astype(jnp.int32), axis=1)
    valid = (w_idx[None, :] < count[:, None]).reshape(slots)
    tok_slot = jnp.sum(
        jnp.where((pslot[None, :] == r_idx[:, None]) & valid[None, :], s_idx[None, :], 0),
        axis=1,
    )

    doc = seg_doc[me]
    start = jnp.min(jnp.where(seg_doc == doc, o_idx, n))
    score_scale = dh ** (-0.5)
    causal = r_idx[:, None] >= r_idx[None, :]
    head_count = lax.axis_size("head")
    out_cols = out_weight.shape[1]
    bounds = [0, heads // 2, heads]
    weight_rows = out_weight.reshape(head_count, heads, dh, out_cols)
    gate_all = jax.nn.sigmoid(mem_gate)
    shifts = []
    step = 1
    while step < n:
        shifts.append(step)
        step *= 2

    def dispatch(source):
        buffer = jnp.take(source, slot_row, axis=0, mode="clip").reshape(n, cap, width)
        got = lax.all_to_all(buffer, "ctx", 0, 0, tiled=True).reshape(slots, width)
        return jnp.take(got, tok_slot, axis=0, mode="clip").reshape(seg, heads, dh)

    key_all = dispatch(keys)
    value_all = dispatch(values)

    def memory_terms(first, last):
        key_feat = feature(key_all[:, first:last].astype(f32))
        delta_m = jnp.einsum(
            "khd,khe->hde", key_feat, value_all[:, first:last].astype(f32), precision=highest
        )
        delta_z = jnp.sum(key_feat, axis=0)
        return jnp.concatenate([delta_m, delta_z[:, None, :]], axis=1)

    first_delta = memory_terms(bounds[0], bounds[1])
    queries_after, first_delta = lax.optimization_barrier((queries, first_delta))
    query_all = dispatch(queries_after)

    def local_attention(query_part, key_part, value_part):
        scores = jnp.einsum(
            "qhd,khd->hqk", query_part, key_part, preferred_element_type=f32
        ) * score_scale
        scores = jnp.where(causal[None], scores, -1e30)
        row_max = jnp.max(scores, axis=-1, keepdims=True)
        weights = jnp.exp(scores - row_max)
        probabilities = (weights / jnp.sum(weights, axis=-1, keepdims=True)).astype(bf16)
        return jnp.einsum(
            "hqk,khd->qhd", probabilities, value_part, preferred_element_type=f32
        )

    def one_group(g, hold):
        first, last = bounds[g], bounds[g + 1]
        group_heads = last - first
        group_width = group_heads * dh
        skip = 2 if g == 0 and len(shifts) > 2 else 0
        slots_used = len(shifts) - skip
        cuts = [0] * skip + [round(group_heads * i / slots_used) for i in range(slots_used + 1)]
        key_heads = key_all[:, first:last]
        value_heads = value_all[:, first:last]
        query_heads = query_all[:, first:last]

        delta = first_delta if g == 0 else memory_terms(first, last)
        if hold is not None:
            delta, _ = lax.optimization_barrier((delta, hold))

        pieces = []
        total = delta
        for k, step in enumerate(shifts):
            lo, hi = cuts[k], cuts[k + 1]
            operands = None
            if hi > lo:
                total, operands = lax.optimization_barrier(
                    (total, (query_heads[:, lo:hi], key_heads[:, lo:hi], value_heads[:, lo:hi]))
                )
            perm = [(j, j + step) for j in range(n - step)]
            got = lax.ppermute(total, "ctx", perm)
            if hi > lo:
                piece = local_attention(*operands)
                got, piece = lax.optimization_barrier((got, piece))
                pieces.append(piece)
            total = total + jnp.where(me - step >= start, got, jnp.zeros_like(got))
        local_out = jnp.concatenate(pieces, axis=1)
        memory = total - delta
        mem_m = memory[:, :dh, :]
        mem_z = memory[:, dh, :]

        query_feat = feature(query_heads.astype(f32))
        numerator = jnp.einsum("qhd,hde->qhe", query_feat, mem_m, precision=highest)
        denominator = jnp.einsum("qhd,hd->qh", query_feat, mem_z, precision=highest)
        recalled = numerator / jnp.maximum(denominator, 1.0)[..., None]
        gate_value = gate_all[first:last][None, :, None]
        combined = (
            (gate_value * recalled + (1.0 - gate_value) * local_out)
            .astype(bf16)
            .reshape(seg, group_width)
        )

        outgoing = jnp.take(combined, pslot, axis=0, mode="clip").reshape(n, cap, group_width)
        incoming = lax.all_to_all(outgoing, "ctx", 0, 0, tiled=True).reshape(slots, group_width)
        rows = jnp.take(incoming, send_slot, axis=0, mode="clip")
        gathered = lax.all_gather(rows, "head", axis=1, tiled=True)
        part = jnp.dot(
            gathered,
            weight_rows[:, first:last].reshape(head_count * group_width, out_cols),
            preferred_element_type=f32,
        )
        return part, combined

    summed, hold = one_group(0, None)
    for g in range(1, len(bounds) - 1):
        part, hold = one_group(g, hold)
        summed = summed + part
    return summed.astype(bf16)


def solution(mesh):
    return jax.shard_map(
        per_device,
        mesh=mesh,
        in_specs=(
            P("ctx", "head"),
            P("ctx", "head"),
            P("ctx", "head"),
            P(),
            P(),
            P("head"),
            P(None, "head"),
        ),
        out_specs=P("ctx", "head"),
        check_vma=False,
    )
```

```python
import jax
import jax.numpy as jnp
from jax import lax
from jax.sharding import PartitionSpec as P


def feature(inputs):
    return jax.nn.elu(inputs) + 1.0


def per_device(queries, keys, values, row_target, seg_doc, mem_gate, out_weight):
    highest = lax.Precision.HIGHEST
    f32, bf16 = jnp.float32, jnp.bfloat16
    n = lax.axis_size("ctx")
    me = lax.axis_index("ctx")
    seg, width = queries.shape
    heads = mem_gate.shape[0]
    dh = width // heads
    cap = seg // n + (seg // n) // 2
    slots = n * cap

    targets = row_target.reshape(n, seg)
    r_idx = jnp.arange(seg, dtype=jnp.int32)
    o_idx = jnp.arange(n, dtype=jnp.int32)
    s_idx = jnp.arange(slots, dtype=jnp.int32)
    w_idx = jnp.arange(cap, dtype=jnp.int32)
    lower = (r_idx[None, :] < r_idx[:, None]).astype(bf16)

    mine = lax.dynamic_index_in_dim(targets, me, 0, keepdims=False)
    owner = mine // seg
    match = (owner[:, None] == o_idx[None, :]).astype(bf16)
    before = jnp.dot(lower, match, preferred_element_type=f32)
    within = jnp.sum(jnp.where(match > 0, before, 0.0), axis=1).astype(jnp.int32)
    send_slot = owner * cap + within
    slot_row = jnp.sum(
        jnp.where(send_slot[None, :] == s_idx[:, None], r_idx[None, :], 0), axis=1
    )

    arrived = (targets // seg) == me
    rank = jnp.dot(arrived.astype(bf16), lower.T, preferred_element_type=f32).astype(jnp.int32)
    hit = arrived[:, None, :] & (rank[:, None, :] == w_idx[None, :, None])
    pslot = jnp.sum(jnp.where(hit, (targets % seg)[:, None, :], 0), axis=2).reshape(slots)
    count = jnp.sum(arrived.astype(jnp.int32), axis=1)
    valid = (w_idx[None, :] < count[:, None]).reshape(slots)
    tok_slot = jnp.sum(
        jnp.where((pslot[None, :] == r_idx[:, None]) & valid[None, :], s_idx[None, :], 0),
        axis=1,
    )

    doc = seg_doc[me]
    start = jnp.min(jnp.where(seg_doc == doc, o_idx, n))
    score_scale = dh ** (-0.5)
    causal = r_idx[:, None] >= r_idx[None, :]
    head_count = lax.axis_size("head")
    out_cols = out_weight.shape[1]
    bounds = [0, heads // 2, heads]
    weight_rows = out_weight.reshape(head_count, heads, dh, out_cols)
    gate_all = jax.nn.sigmoid(mem_gate)
    shifts = []
    step = 1
    while step < n:
        shifts.append(step)
        step *= 2

    def dispatch(source):
        buffer = jnp.take(source, slot_row, axis=0, mode="clip").reshape(n, cap, width)
        got = lax.all_to_all(buffer, "ctx", 0, 0, tiled=True).reshape(slots, width)
        return jnp.take(got, tok_slot, axis=0, mode="clip").reshape(seg, heads, dh)

    key_all = dispatch(keys)
    value_all = dispatch(values)
    query_all = dispatch(queries)

    def local_attention(query_part, key_part, value_part):
        scores = jnp.einsum(
            "qhd,khd->hqk", query_part, key_part, preferred_element_type=f32
        ) * score_scale
        scores = jnp.where(causal[None], scores, -1e30)
        row_max = jnp.max(scores, axis=-1, keepdims=True)
        weights = jnp.exp(scores - row_max)
        probabilities = (weights / jnp.sum(weights, axis=-1, keepdims=True)).astype(bf16)
        return jnp.einsum(
            "hqk,khd->qhd", probabilities, value_part, preferred_element_type=f32
        )

    def one_group(g, hold):
        first, last = bounds[g], bounds[g + 1]
        group_heads = last - first
        group_width = group_heads * dh
        cuts = [first + round(group_heads * i / len(shifts)) for i in range(len(shifts) + 1)]
        cuts = [c - first for c in cuts]
        key_heads = key_all[:, first:last]
        value_heads = value_all[:, first:last]
        query_heads = query_all[:, first:last]

        key_feat = feature(key_heads.astype(f32))
        delta_m = jnp.einsum(
            "khd,khe->hde", key_feat, value_heads.astype(f32), precision=highest
        )
        delta_z = jnp.sum(key_feat, axis=0)
        delta = jnp.concatenate([delta_m, delta_z[:, None, :]], axis=1)
        if hold is not None:
            delta, _ = lax.optimization_barrier((delta, hold))

        pieces = []
        total = delta
        for k, step in enumerate(shifts):
            lo, hi = cuts[k], cuts[k + 1]
            total, operands = lax.optimization_barrier(
                (total, (query_heads[:, lo:hi], key_heads[:, lo:hi], value_heads[:, lo:hi]))
            )
            perm = [(j, j + step) for j in range(n - step)]
            got = lax.ppermute(total, "ctx", perm)
            if hi > lo:
                piece = local_attention(*operands)
                got, piece = lax.optimization_barrier((got, piece))
                pieces.append(piece)
            total = total + jnp.where(me - step >= start, got, jnp.zeros_like(got))
        local_out = jnp.concatenate(pieces, axis=1)
        memory = total - delta
        mem_m = memory[:, :dh, :]
        mem_z = memory[:, dh, :]

        query_feat = feature(query_heads.astype(f32))
        numerator = jnp.einsum("qhd,hde->qhe", query_feat, mem_m, precision=highest)
        denominator = jnp.einsum("qhd,hd->qh", query_feat, mem_z, precision=highest)
        recalled = numerator / jnp.maximum(denominator, 1.0)[..., None]
        gate_value = gate_all[first:last][None, :, None]
        combined = (
            (gate_value * recalled + (1.0 - gate_value) * local_out)
            .astype(bf16)
            .reshape(seg, group_width)
        )

        outgoing = jnp.take(combined, pslot, axis=0, mode="clip").reshape(n, cap, group_width)
        incoming = lax.all_to_all(outgoing, "ctx", 0, 0, tiled=True).reshape(slots, group_width)
        rows = jnp.take(incoming, send_slot, axis=0, mode="clip")
        if last == heads:
            spread = jnp.broadcast_to(rows[None], (head_count, seg, group_width))
            blocks = lax.all_to_all(spread, "head", 0, 0, tiled=True)
            part = jnp.einsum(
                "hrc,hcd->rd",
                blocks,
                weight_rows[:, first:last].reshape(head_count, group_width, out_cols),
                preferred_element_type=f32,
            )
        else:
            gathered = lax.all_gather(rows, "head", axis=1, tiled=True)
            part = jnp.dot(
                gathered,
                weight_rows[:, first:last].reshape(head_count * group_width, out_cols),
                preferred_element_type=f32,
            )
        return part, combined

    summed, hold = one_group(0, None)
    for g in range(1, len(bounds) - 1):
        part, hold = one_group(g, hold)
        summed = summed + part
    return summed.astype(bf16)


def solution(mesh):
    return jax.shard_map(
        per_device,
        mesh=mesh,
        in_specs=(
            P("ctx", "head"),
            P("ctx", "head"),
            P("ctx", "head"),
            P(),
            P(),
            P("head"),
            P(None, "head"),
        ),
        out_specs=P("ctx", "head"),
        check_vma=False,
    )
```

```python
import jax
import jax.numpy as jnp
from jax import lax
from jax.sharding import PartitionSpec as P


def feature(inputs):
    return jax.nn.elu(inputs) + 1.0


def per_device(queries, keys, values, row_target, seg_doc, mem_gate, out_weight):
    highest = lax.Precision.HIGHEST
    f32, bf16 = jnp.float32, jnp.bfloat16
    n = lax.axis_size("ctx")
    me = lax.axis_index("ctx")
    seg, width = queries.shape
    heads = mem_gate.shape[0]
    dh = width // heads
    cap = seg // n + (seg // n) // 2
    slots = n * cap

    targets = row_target.reshape(n, seg)
    r_idx = jnp.arange(seg, dtype=jnp.int32)
    o_idx = jnp.arange(n, dtype=jnp.int32)
    s_idx = jnp.arange(slots, dtype=jnp.int32)
    w_idx = jnp.arange(cap, dtype=jnp.int32)
    lower = (r_idx[None, :] < r_idx[:, None]).astype(bf16)

    mine = lax.dynamic_index_in_dim(targets, me, 0, keepdims=False)
    owner = mine // seg
    match = (owner[:, None] == o_idx[None, :]).astype(bf16)
    before = jnp.dot(lower, match, preferred_element_type=f32)
    within = jnp.sum(jnp.where(match > 0, before, 0.0), axis=1).astype(jnp.int32)
    send_slot = owner * cap + within
    slot_row = jnp.sum(
        jnp.where(send_slot[None, :] == s_idx[:, None], r_idx[None, :], 0), axis=1
    )

    arrived = (targets // seg) == me
    rank = jnp.dot(arrived.astype(bf16), lower.T, preferred_element_type=f32).astype(jnp.int32)
    hit = arrived[:, None, :] & (rank[:, None, :] == w_idx[None, :, None])
    pslot = jnp.sum(jnp.where(hit, (targets % seg)[:, None, :], 0), axis=2).reshape(slots)
    count = jnp.sum(arrived.astype(jnp.int32), axis=1)
    valid = (w_idx[None, :] < count[:, None]).reshape(slots)
    tok_slot = jnp.sum(
        jnp.where((pslot[None, :] == r_idx[:, None]) & valid[None, :], s_idx[None, :], 0),
        axis=1,
    )

    doc = seg_doc[me]
    start = jnp.min(jnp.where(seg_doc == doc, o_idx, n))
    score_scale = dh ** (-0.5)
    causal = r_idx[:, None] >= r_idx[None, :]
    head_count = lax.axis_size("head")
    out_cols = out_weight.shape[1]
    bounds = [0, heads // 2, heads]
    weight_rows = out_weight.reshape(head_count, heads, dh, out_cols)
    gate_all = jax.nn.sigmoid(mem_gate)
    shifts = []
    step = 1
    while step < n:
        shifts.append(step)
        step *= 2

    def dispatch(source):
        buffer = jnp.take(source, slot_row, axis=0, mode="clip").reshape(n, cap, width)
        got = lax.all_to_all(buffer, "ctx", 0, 0, tiled=True).reshape(slots, width)
        return jnp.take(got, tok_slot, axis=0, mode="clip").reshape(seg, heads, dh)

    key_all = dispatch(keys)
    value_all = dispatch(values)
    query_all = dispatch(queries)

    def local_attention(query_part, key_part, value_part):
        scores = jnp.einsum(
            "qhd,khd->hqk", query_part, key_part, preferred_element_type=f32
        ) * score_scale
        scores = jnp.where(causal[None], scores, -1e30)
        row_max = jnp.max(scores, axis=-1, keepdims=True)
        weights = jnp.exp(scores - row_max)
        probabilities = (weights / jnp.sum(weights, axis=-1, keepdims=True)).astype(bf16)
        return jnp.einsum(
            "hqk,khd->qhd", probabilities, value_part, preferred_element_type=f32
        )

    def one_group(g, hold):
        first, last = bounds[g], bounds[g + 1]
        group_heads = last - first
        group_width = group_heads * dh
        cuts = [first + round(group_heads * i / len(shifts)) for i in range(len(shifts) + 1)]
        cuts = [c - first for c in cuts]
        key_heads = key_all[:, first:last]
        value_heads = value_all[:, first:last]
        query_heads = query_all[:, first:last]

        key_feat = feature(key_heads.astype(f32))
        delta_m = jnp.einsum(
            "khd,khe->hde", key_feat, value_heads.astype(f32), precision=highest
        )
        delta_z = jnp.sum(key_feat, axis=0)
        delta = jnp.concatenate([delta_m, delta_z[:, None, :]], axis=1)
        if hold is not None:
            delta, _ = lax.optimization_barrier((delta, hold))

        pieces = []
        total = delta
        for k, step in enumerate(shifts):
            lo, hi = cuts[k], cuts[k + 1]
            total, operands = lax.optimization_barrier(
                (total, (query_heads[:, lo:hi], key_heads[:, lo:hi], value_heads[:, lo:hi]))
            )
            perm = [(j, j + step) for j in range(n - step)]
            got = lax.ppermute(total, "ctx", perm)
            if hi > lo:
                piece = local_attention(*operands)
                got, piece = lax.optimization_barrier((got, piece))
                pieces.append(piece)
            total = total + jnp.where(me - step >= start, got, jnp.zeros_like(got))
        local_out = jnp.concatenate(pieces, axis=1)
        memory = total - delta
        mem_m = memory[:, :dh, :]
        mem_z = memory[:, dh, :]

        query_feat = feature(query_heads.astype(f32))
        numerator = jnp.einsum("qhd,hde->qhe", query_feat, mem_m, precision=highest)
        denominator = jnp.einsum("qhd,hd->qh", query_feat, mem_z, precision=highest)
        recalled = numerator / jnp.maximum(denominator, 1.0)[..., None]
        gate_value = gate_all[first:last][None, :, None]
        combined = (
            (gate_value * recalled + (1.0 - gate_value) * local_out)
            .astype(bf16)
            .reshape(seg, group_width)
        )

        outgoing = jnp.take(combined, pslot, axis=0, mode="clip").reshape(n, cap, group_width)
        incoming = lax.all_to_all(outgoing, "ctx", 0, 0, tiled=True).reshape(slots, group_width)
        rows = jnp.take(incoming, send_slot, axis=0, mode="clip")
        gathered = lax.all_gather(rows, "head", axis=0, tiled=False)
        part = jnp.einsum(
            "hrc,hcd->rd",
            gathered,
            weight_rows[:, first:last].reshape(head_count, group_width, out_cols),
            preferred_element_type=f32,
        )
        return part, combined

    summed, hold = one_group(0, None)
    for g in range(1, len(bounds) - 1):
        part, hold = one_group(g, hold)
        summed = summed + part
    return summed.astype(bf16)


def solution(mesh):
    return jax.shard_map(
        per_device,
        mesh=mesh,
        in_specs=(
            P("ctx", "head"),
            P("ctx", "head"),
            P("ctx", "head"),
            P(),
            P(),
            P("head"),
            P(None, "head"),
        ),
        out_specs=P("ctx", "head"),
        check_vma=False,
    )
```

```python
import jax
import jax.numpy as jnp
from jax import lax
from jax.sharding import PartitionSpec as P


def feature(inputs):
    return jax.nn.elu(inputs) + 1.0


def per_device(queries, keys, values, row_target, seg_doc, mem_gate, out_weight):
    highest = lax.Precision.HIGHEST
    f32, bf16 = jnp.float32, jnp.bfloat16
    n = lax.axis_size("ctx")
    me = lax.axis_index("ctx")
    seg, width = queries.shape
    heads = mem_gate.shape[0]
    dh = width // heads
    cap = seg // n + (seg // n) // 2
    slots = n * cap

    targets = row_target.reshape(n, seg)
    r_idx = jnp.arange(seg, dtype=jnp.int32)
    o_idx = jnp.arange(n, dtype=jnp.int32)
    s_idx = jnp.arange(slots, dtype=jnp.int32)
    w_idx = jnp.arange(cap, dtype=jnp.int32)
    lower = (r_idx[None, :] < r_idx[:, None]).astype(bf16)

    mine = lax.dynamic_index_in_dim(targets, me, 0, keepdims=False)
    owner = mine // seg
    match = (owner[:, None] == o_idx[None, :]).astype(bf16)
    before = jnp.dot(lower, match, preferred_element_type=f32)
    within = jnp.sum(jnp.where(match > 0, before, 0.0), axis=1).astype(jnp.int32)
    send_slot = owner * cap + within
    slot_row = jnp.sum(
        jnp.where(send_slot[None, :] == s_idx[:, None], r_idx[None, :], 0), axis=1
    )

    arrived = (targets // seg) == me
    rank = jnp.dot(arrived.astype(bf16), lower.T, preferred_element_type=f32).astype(jnp.int32)
    hit = arrived[:, None, :] & (rank[:, None, :] == w_idx[None, :, None])
    pslot = jnp.sum(jnp.where(hit, (targets % seg)[:, None, :], 0), axis=2).reshape(slots)
    count = jnp.sum(arrived.astype(jnp.int32), axis=1)
    valid = (w_idx[None, :] < count[:, None]).reshape(slots)
    tok_slot = jnp.sum(
        jnp.where((pslot[None, :] == r_idx[:, None]) & valid[None, :], s_idx[None, :], 0),
        axis=1,
    )

    doc = seg_doc[me]
    start = jnp.min(jnp.where(seg_doc == doc, o_idx, n))
    score_scale = dh ** (-0.5)
    causal = r_idx[:, None] >= r_idx[None, :]
    head_count = lax.axis_size("head")
    out_cols = out_weight.shape[1]
    bounds = [0, heads // 2, heads]
    weight_rows = out_weight.reshape(head_count, heads, dh, out_cols)
    gate_all = jax.nn.sigmoid(mem_gate)
    shifts = []
    step = 1
    while step < n:
        shifts.append(step)
        step *= 2

    def dispatch(source):
        buffer = jnp.take(source, slot_row, axis=0, mode="clip").reshape(n, cap, width)
        got = lax.all_to_all(buffer, "ctx", 0, 0, tiled=True).reshape(slots, width)
        return jnp.take(got, tok_slot, axis=0, mode="clip").reshape(seg, heads, dh)

    key_all = dispatch(keys)
    value_all = dispatch(values)
    query_all = dispatch(queries)

    def local_attention(query_part, key_part, value_part):
        scores = jnp.einsum(
            "qhd,khd->hqk", query_part, key_part, preferred_element_type=f32
        ) * score_scale
        scores = jnp.where(causal[None], scores, -1e30)
        row_max = jnp.max(scores, axis=-1, keepdims=True)
        weights = jnp.exp(scores - row_max)
        probabilities = (weights / jnp.sum(weights, axis=-1, keepdims=True)).astype(bf16)
        return jnp.einsum(
            "hqk,khd->qhd", probabilities, value_part, preferred_element_type=f32
        )

    key_feat = feature(key_all.astype(f32))
    delta_m = jnp.einsum(
        "khd,khe->hde", key_feat, value_all.astype(f32), precision=highest
    )
    delta_z = jnp.sum(key_feat, axis=0)
    delta = jnp.concatenate([delta_m, delta_z[:, None, :]], axis=1)

    first_heads = bounds[1]
    cuts = [round(first_heads * i / len(shifts)) for i in range(len(shifts) + 1)]
    pieces = []
    total = delta
    for k, step in enumerate(shifts):
        lo, hi = cuts[k], cuts[k + 1]
        operands = None
        if hi > lo:
            total, operands = lax.optimization_barrier(
                (total, (query_all[:, lo:hi], key_all[:, lo:hi], value_all[:, lo:hi]))
            )
        perm = [(j, j + step) for j in range(n - step)]
        got = lax.ppermute(total, "ctx", perm)
        if hi > lo:
            piece = local_attention(*operands)
            got, piece = lax.optimization_barrier((got, piece))
            pieces.append(piece)
        total = total + jnp.where(me - step >= start, got, jnp.zeros_like(got))
    memory = total - delta
    first_local = jnp.concatenate(pieces, axis=1)

    def one_group(g, hold):
        first, last = bounds[g], bounds[g + 1]
        group_heads = last - first
        group_width = group_heads * dh
        query_heads = query_all[:, first:last]
        if g == 0:
            local_out = first_local
        else:
            operands = (query_heads, key_all[:, first:last], value_all[:, first:last])
            if hold is not None:
                operands, _ = lax.optimization_barrier((operands, hold))
            local_out = local_attention(*operands)
        mem_m = memory[first:last, :dh, :]
        mem_z = memory[first:last, dh, :]

        query_feat = feature(query_heads.astype(f32))
        numerator = jnp.einsum("qhd,hde->qhe", query_feat, mem_m, precision=highest)
        denominator = jnp.einsum("qhd,hd->qh", query_feat, mem_z, precision=highest)
        recalled = numerator / jnp.maximum(denominator, 1.0)[..., None]
        gate_value = gate_all[first:last][None, :, None]
        combined = (
            (gate_value * recalled + (1.0 - gate_value) * local_out)
            .astype(bf16)
            .reshape(seg, group_width)
        )

        outgoing = jnp.take(combined, pslot, axis=0, mode="clip").reshape(n, cap, group_width)
        incoming = lax.all_to_all(outgoing, "ctx", 0, 0, tiled=True).reshape(slots, group_width)
        rows = jnp.take(incoming, send_slot, axis=0, mode="clip")
        gathered = lax.all_gather(rows, "head", axis=1, tiled=True)
        part = jnp.dot(
            gathered,
            weight_rows[:, first:last].reshape(head_count * group_width, out_cols),
            preferred_element_type=f32,
        )
        return part, outgoing

    summed, hold = one_group(0, None)
    for g in range(1, len(bounds) - 1):
        part, hold = one_group(g, hold)
        summed = summed + part
    return summed.astype(bf16)


def solution(mesh):
    return jax.shard_map(
        per_device,
        mesh=mesh,
        in_specs=(
            P("ctx", "head"),
            P("ctx", "head"),
            P("ctx", "head"),
            P(),
            P(),
            P("head"),
            P(None, "head"),
        ),
        out_specs=P("ctx", "head"),
        check_vma=False,
    )
```

```python
import jax
import jax.numpy as jnp
from jax import lax
from jax.sharding import PartitionSpec as P


def feature(inputs):
    return jax.nn.elu(inputs) + 1.0


def per_device(queries, keys, values, row_target, seg_doc, mem_gate, out_weight):
    highest = lax.Precision.HIGHEST
    f32, bf16 = jnp.float32, jnp.bfloat16
    n = lax.axis_size("ctx")
    me = lax.axis_index("ctx")
    seg, width = queries.shape
    heads = mem_gate.shape[0]
    dh = width // heads
    cap = seg // n + (seg // n) // 2
    slots = n * cap

    targets = row_target.reshape(n, seg)
    r_idx = jnp.arange(seg, dtype=jnp.int32)
    o_idx = jnp.arange(n, dtype=jnp.int32)
    s_idx = jnp.arange(slots, dtype=jnp.int32)
    w_idx = jnp.arange(cap, dtype=jnp.int32)
    lower = (r_idx[None, :] < r_idx[:, None]).astype(bf16)

    mine = lax.dynamic_index_in_dim(targets, me, 0, keepdims=False)
    owner = mine // seg
    match = (owner[:, None] == o_idx[None, :]).astype(bf16)
    before = jnp.dot(lower, match, preferred_element_type=f32)
    within = jnp.sum(jnp.where(match > 0, before, 0.0), axis=1).astype(jnp.int32)
    send_slot = owner * cap + within
    slot_row = jnp.sum(
        jnp.where(send_slot[None, :] == s_idx[:, None], r_idx[None, :], 0), axis=1
    )

    arrived = (targets // seg) == me
    rank = jnp.dot(arrived.astype(bf16), lower.T, preferred_element_type=f32).astype(jnp.int32)
    hit = arrived[:, None, :] & (rank[:, None, :] == w_idx[None, :, None])
    pslot = jnp.sum(jnp.where(hit, (targets % seg)[:, None, :], 0), axis=2).reshape(slots)
    count = jnp.sum(arrived.astype(jnp.int32), axis=1)
    valid = (w_idx[None, :] < count[:, None]).reshape(slots)
    tok_slot = jnp.sum(
        jnp.where((pslot[None, :] == r_idx[:, None]) & valid[None, :], s_idx[None, :], 0),
        axis=1,
    )

    doc = seg_doc[me]
    start = jnp.min(jnp.where(seg_doc == doc, o_idx, n))
    score_scale = dh ** (-0.5)
    causal = r_idx[:, None] >= r_idx[None, :]
    head_count = lax.axis_size("head")
    out_cols = out_weight.shape[1]
    bounds = [0, heads // 2, heads]
    weight_rows = out_weight.reshape(head_count, heads, dh, out_cols)
    gate_all = jax.nn.sigmoid(mem_gate)
    shifts = []
    step = 1
    while step < n:
        shifts.append(step)
        step *= 2

    def dispatch(source):
        buffer = jnp.take(source, slot_row, axis=0, mode="clip").reshape(n, cap, width)
        got = lax.all_to_all(buffer, "ctx", 0, 0, tiled=True).reshape(slots, width)
        return jnp.take(got, tok_slot, axis=0, mode="clip").reshape(seg, heads, dh)

    key_all = dispatch(keys)
    value_all = dispatch(values)
    query_all = dispatch(queries)

    def local_attention(query_part, key_part, value_part):
        scores = jnp.einsum(
            "qhd,khd->hqk", query_part, key_part, preferred_element_type=f32
        ) * score_scale
        scores = jnp.where(causal[None], scores, -1e30)
        row_max = jnp.max(scores, axis=-1, keepdims=True)
        weights = jnp.exp(scores - row_max)
        probabilities = (weights / jnp.sum(weights, axis=-1, keepdims=True)).astype(bf16)
        return jnp.einsum(
            "hqk,khd->qhd", probabilities, value_part, preferred_element_type=f32
        )

    def one_group(g, hold):
        first, last = bounds[g], bounds[g + 1]
        group_heads = last - first
        group_width = group_heads * dh
        cuts = [first + round(group_heads * i / len(shifts)) for i in range(len(shifts) + 1)]
        cuts = [c - first for c in cuts]
        key_heads = key_all[:, first:last]
        value_heads = value_all[:, first:last]
        query_heads = query_all[:, first:last]

        key_feat = feature(key_heads.astype(f32))
        delta_m = jnp.einsum(
            "khd,khe->hde", key_feat, value_heads.astype(f32), precision=highest
        )
        delta_z = jnp.sum(key_feat, axis=0)
        delta = jnp.concatenate([delta_m, delta_z[:, None, :]], axis=1)
        if hold is not None:
            delta, _ = lax.optimization_barrier((delta, hold))

        pieces = []
        total = delta
        for k, step in enumerate(shifts):
            lo, hi = cuts[k], cuts[k + 1]
            total, (q_pass, k_pass, v_pass) = lax.optimization_barrier(
                (total, (query_all, key_all, value_all))
            )
            perm = [(j, j + step) for j in range(n - step)]
            got = lax.ppermute(total, "ctx", perm)
            if hi > lo:
                piece = local_attention(
                    q_pass[:, first + lo:first + hi],
                    k_pass[:, first + lo:first + hi],
                    v_pass[:, first + lo:first + hi],
                )
                got, piece = lax.optimization_barrier((got, piece))
                pieces.append(piece)
            total = total + jnp.where(me - step >= start, got, jnp.zeros_like(got))
        local_out = jnp.concatenate(pieces, axis=1)
        memory = total - delta
        mem_m = memory[:, :dh, :]
        mem_z = memory[:, dh, :]

        query_feat = feature(query_heads.astype(f32))
        numerator = jnp.einsum("qhd,hde->qhe", query_feat, mem_m, precision=highest)
        denominator = jnp.einsum("qhd,hd->qh", query_feat, mem_z, precision=highest)
        recalled = numerator / jnp.maximum(denominator, 1.0)[..., None]
        gate_value = gate_all[first:last][None, :, None]
        combined = (
            (gate_value * recalled + (1.0 - gate_value) * local_out)
            .astype(bf16)
            .reshape(seg, group_width)
        )

        outgoing = jnp.take(combined, pslot, axis=0, mode="clip").reshape(n, cap, group_width)
        incoming = lax.all_to_all(outgoing, "ctx", 0, 0, tiled=True).reshape(slots, group_width)
        rows = jnp.take(incoming, send_slot, axis=0, mode="clip")
        gathered = lax.all_gather(rows, "head", axis=1, tiled=True)
        part = jnp.dot(
            gathered,
            weight_rows[:, first:last].reshape(head_count * group_width, out_cols),
            preferred_element_type=f32,
        )
        return part, combined

    summed, hold = one_group(0, None)
    for g in range(1, len(bounds) - 1):
        part, hold = one_group(g, hold)
        summed = summed + part
    return summed.astype(bf16)


def solution(mesh):
    return jax.shard_map(
        per_device,
        mesh=mesh,
        in_specs=(
            P("ctx", "head"),
            P("ctx", "head"),
            P("ctx", "head"),
            P(),
            P(),
            P("head"),
            P(None, "head"),
        ),
        out_specs=P("ctx", "head"),
        check_vma=False,
    )
```

```python
import jax
import jax.numpy as jnp
from jax import lax
from jax.sharding import PartitionSpec as P


def feature(inputs):
    return jax.nn.elu(inputs) + 1.0


def per_device(queries, keys, values, row_target, seg_doc, mem_gate, out_weight):
    highest = lax.Precision.HIGHEST
    f32, bf16 = jnp.float32, jnp.bfloat16
    n = lax.axis_size("ctx")
    me = lax.axis_index("ctx")
    seg, width = queries.shape
    heads = mem_gate.shape[0]
    dh = width // heads
    cap = seg // n + (seg // n) // 2
    slots = n * cap

    targets = row_target.reshape(n, seg)
    r_idx = jnp.arange(seg, dtype=jnp.int32)
    o_idx = jnp.arange(n, dtype=jnp.int32)
    s_idx = jnp.arange(slots, dtype=jnp.int32)
    w_idx = jnp.arange(cap, dtype=jnp.int32)
    lower = (r_idx[None, :] < r_idx[:, None]).astype(bf16)

    mine = lax.dynamic_index_in_dim(targets, me, 0, keepdims=False)
    owner = mine // seg
    match = (owner[:, None] == o_idx[None, :]).astype(bf16)
    before = jnp.dot(lower, match, preferred_element_type=f32)
    within = jnp.sum(jnp.where(match > 0, before, 0.0), axis=1).astype(jnp.int32)
    send_slot = owner * cap + within
    slot_row = jnp.sum(
        jnp.where(send_slot[None, :] == s_idx[:, None], r_idx[None, :], 0), axis=1
    )

    arrived = (targets // seg) == me
    rank = jnp.dot(arrived.astype(bf16), lower.T, preferred_element_type=f32).astype(jnp.int32)
    hit = arrived[:, None, :] & (rank[:, None, :] == w_idx[None, :, None])
    pslot = jnp.sum(jnp.where(hit, (targets % seg)[:, None, :], 0), axis=2).reshape(slots)
    count = jnp.sum(arrived.astype(jnp.int32), axis=1)
    valid = (w_idx[None, :] < count[:, None]).reshape(slots)
    tok_slot = jnp.sum(
        jnp.where((pslot[None, :] == r_idx[:, None]) & valid[None, :], s_idx[None, :], 0),
        axis=1,
    )

    doc = seg_doc[me]
    start = jnp.min(jnp.where(seg_doc == doc, o_idx, n))
    score_scale = dh ** (-0.5)
    causal = r_idx[:, None] >= r_idx[None, :]
    head_count = lax.axis_size("head")
    out_cols = out_weight.shape[1]
    bounds = [0, heads // 2, heads]
    weight_rows = out_weight.reshape(head_count, heads, dh, out_cols)
    gate_all = jax.nn.sigmoid(mem_gate)
    shifts = []
    step = 1
    while step < n:
        shifts.append(step)
        step *= 2

    def dispatch(source):
        buffer = jnp.take(source, slot_row, axis=0, mode="clip").reshape(n, cap, width)
        got = lax.all_to_all(buffer, "ctx", 0, 0, tiled=True).reshape(slots, width)
        return jnp.take(got, tok_slot, axis=0, mode="clip").reshape(seg, heads, dh)

    key_all = dispatch(keys)
    value_all = dispatch(values)
    query_all = dispatch(queries)

    def local_attention(query_part, key_part, value_part):
        scores = jnp.einsum(
            "qhd,khd->hqk", query_part, key_part, preferred_element_type=f32
        ) * score_scale
        scores = jnp.where(causal[None], scores, -1e30)
        row_max = jnp.max(scores, axis=-1, keepdims=True)
        weights = jnp.exp(scores - row_max)
        probabilities = (weights / jnp.sum(weights, axis=-1, keepdims=True)).astype(bf16)
        return jnp.einsum(
            "hqk,khd->qhd", probabilities, value_part, preferred_element_type=f32
        )

    def one_group(g, hold):
        first, last = bounds[g], bounds[g + 1]
        group_heads = last - first
        group_width = group_heads * dh
        skip = 1 if g == 0 and len(shifts) > 1 else 0
        used = len(shifts) - skip
        cuts = [0] * skip + [round(group_heads * i / used) for i in range(used + 1)]
        key_heads = key_all[:, first:last]
        value_heads = value_all[:, first:last]
        query_heads = query_all[:, first:last]

        key_feat = feature(key_heads.astype(f32))
        delta_m = jnp.einsum(
            "khd,khe->hde", key_feat, value_heads.astype(f32), precision=highest
        )
        delta_z = jnp.sum(key_feat, axis=0)
        delta = jnp.concatenate([delta_m, delta_z[:, None, :]], axis=1)
        if hold is not None:
            delta, _ = lax.optimization_barrier((delta, hold))

        pieces = []
        total = delta
        for k, step in enumerate(shifts):
            lo, hi = cuts[k], cuts[k + 1]
            operands = None
            if hi > lo:
                total, operands = lax.optimization_barrier(
                    (total, (query_heads[:, lo:hi], key_heads[:, lo:hi], value_heads[:, lo:hi]))
                )
            perm = [(j, j + step) for j in range(n - step)]
            got = lax.ppermute(total, "ctx", perm)
            if hi > lo:
                piece = local_attention(*operands)
                got, piece = lax.optimization_barrier((got, piece))
                pieces.append(piece)
            total = total + jnp.where(me - step >= start, got, jnp.zeros_like(got))
        local_out = jnp.concatenate(pieces, axis=1)
        memory = total - delta
        mem_m = memory[:, :dh, :]
        mem_z = memory[:, dh, :]

        query_feat = feature(query_heads.astype(f32))
        numerator = jnp.einsum("qhd,hde->qhe", query_feat, mem_m, precision=highest)
        denominator = jnp.einsum("qhd,hd->qh", query_feat, mem_z, precision=highest)
        recalled = numerator / jnp.maximum(denominator, 1.0)[..., None]
        gate_value = gate_all[first:last][None, :, None]
        combined = (
            (gate_value * recalled + (1.0 - gate_value) * local_out)
            .astype(bf16)
            .reshape(seg, group_width)
        )

        outgoing = jnp.take(combined, pslot, axis=0, mode="clip").reshape(n, cap, group_width)
        incoming = lax.all_to_all(outgoing, "ctx", 0, 0, tiled=True).reshape(slots, group_width)
        rows = jnp.take(incoming, send_slot, axis=0, mode="clip")
        gathered = lax.all_gather(rows, "head", axis=1, tiled=True)
        part = jnp.dot(
            gathered,
            weight_rows[:, first:last].reshape(head_count * group_width, out_cols),
            preferred_element_type=f32,
        )
        return part, combined

    summed, hold = one_group(0, None)
    for g in range(1, len(bounds) - 1):
        part, hold = one_group(g, hold)
        summed = summed + part
    return summed.astype(bf16)


def solution(mesh):
    return jax.shard_map(
        per_device,
        mesh=mesh,
        in_specs=(
            P("ctx", "head"),
            P("ctx", "head"),
            P("ctx", "head"),
            P(),
            P(),
            P("head"),
            P(None, "head"),
        ),
        out_specs=P("ctx", "head"),
        check_vma=False,
    )
```

```python
import jax
import jax.numpy as jnp
from jax import lax
from jax.sharding import PartitionSpec as P


def feature(inputs):
    return jax.nn.elu(inputs) + 1.0


def per_device(queries, keys, values, row_target, seg_doc, mem_gate, out_weight):
    highest = lax.Precision.HIGHEST
    f32, bf16 = jnp.float32, jnp.bfloat16
    n = lax.axis_size("ctx")
    me = lax.axis_index("ctx")
    seg, width = queries.shape
    heads = mem_gate.shape[0]
    dh = width // heads
    cap = seg // n + (seg // n) // 2
    slots = n * cap

    targets = row_target.reshape(n, seg)
    r_idx = jnp.arange(seg, dtype=jnp.int32)
    o_idx = jnp.arange(n, dtype=jnp.int32)
    s_idx = jnp.arange(slots, dtype=jnp.int32)
    w_idx = jnp.arange(cap, dtype=jnp.int32)
    lower = (r_idx[None, :] < r_idx[:, None]).astype(bf16)

    mine = lax.dynamic_index_in_dim(targets, me, 0, keepdims=False)
    owner = mine // seg
    match = (owner[:, None] == o_idx[None, :]).astype(bf16)
    before = jnp.dot(lower, match, preferred_element_type=f32)
    within = jnp.sum(jnp.where(match > 0, before, 0.0), axis=1).astype(jnp.int32)
    send_slot = owner * cap + within
    slot_row = jnp.sum(
        jnp.where(send_slot[None, :] == s_idx[:, None], r_idx[None, :], 0), axis=1
    )

    arrived = (targets // seg) == me
    rank = jnp.dot(arrived.astype(bf16), lower.T, preferred_element_type=f32).astype(jnp.int32)
    hit = arrived[:, None, :] & (rank[:, None, :] == w_idx[None, :, None])
    pslot = jnp.sum(jnp.where(hit, (targets % seg)[:, None, :], 0), axis=2).reshape(slots)
    count = jnp.sum(arrived.astype(jnp.int32), axis=1)
    valid = (w_idx[None, :] < count[:, None]).reshape(slots)
    tok_slot = jnp.sum(
        jnp.where((pslot[None, :] == r_idx[:, None]) & valid[None, :], s_idx[None, :], 0),
        axis=1,
    )

    doc = seg_doc[me]
    start = jnp.min(jnp.where(seg_doc == doc, o_idx, n))
    score_scale = dh ** (-0.5)
    causal = r_idx[:, None] >= r_idx[None, :]
    head_count = lax.axis_size("head")
    out_cols = out_weight.shape[1]
    bounds = [0, heads - (3 * heads) // 8, heads]
    weight_rows = out_weight.reshape(head_count, heads, dh, out_cols)
    gate_all = jax.nn.sigmoid(mem_gate)
    shifts = []
    step = 1
    while step < n:
        shifts.append(step)
        step *= 2

    def dispatch(source):
        buffer = jnp.take(source, slot_row, axis=0, mode="clip").reshape(n, cap, width)
        got = lax.all_to_all(buffer, "ctx", 0, 0, tiled=True).reshape(slots, width)
        return jnp.take(got, tok_slot, axis=0, mode="clip").reshape(seg, heads, dh)

    key_all = dispatch(keys)
    value_all = dispatch(values)
    query_all = dispatch(queries)

    def local_attention(query_part, key_part, value_part):
        scores = jnp.einsum(
            "qhd,khd->hqk", query_part, key_part, preferred_element_type=f32
        ) * score_scale
        scores = jnp.where(causal[None], scores, -1e30)
        row_max = jnp.max(scores, axis=-1, keepdims=True)
        weights = jnp.exp(scores - row_max)
        probabilities = (weights / jnp.sum(weights, axis=-1, keepdims=True)).astype(bf16)
        return jnp.einsum(
            "hqk,khd->qhd", probabilities, value_part, preferred_element_type=f32
        )

    def one_group(g, hold):
        first, last = bounds[g], bounds[g + 1]
        group_heads = last - first
        group_width = group_heads * dh
        skip = 1 if g == 0 and len(shifts) > 1 else 0
        used = len(shifts) - skip
        cuts = [0] * skip + [round(group_heads * i / used) for i in range(used + 1)]
        key_heads = key_all[:, first:last]
        value_heads = value_all[:, first:last]
        query_heads = query_all[:, first:last]

        key_feat = feature(key_heads.astype(f32))
        delta_m = jnp.einsum(
            "khd,khe->hde", key_feat, value_heads.astype(f32), precision=highest
        )
        delta_z = jnp.sum(key_feat, axis=0)
        delta = jnp.concatenate([delta_m, delta_z[:, None, :]], axis=1)
        if hold is not None:
            delta, _ = lax.optimization_barrier((delta, hold))

        pieces = []
        total = delta
        for k, step in enumerate(shifts):
            lo, hi = cuts[k], cuts[k + 1]
            operands = None
            if hi > lo:
                total, operands = lax.optimization_barrier(
                    (total, (query_heads[:, lo:hi], key_heads[:, lo:hi], value_heads[:, lo:hi]))
                )
            perm = [(j, j + step) for j in range(n - step)]
            got = lax.ppermute(total, "ctx", perm)
            if hi > lo:
                piece = local_attention(*operands)
                got, piece = lax.optimization_barrier((got, piece))
                pieces.append(piece)
            total = total + jnp.where(me - step >= start, got, jnp.zeros_like(got))
        local_out = jnp.concatenate(pieces, axis=1)
        memory = total - delta
        mem_m = memory[:, :dh, :]
        mem_z = memory[:, dh, :]

        query_feat = feature(query_heads.astype(f32))
        numerator = jnp.einsum("qhd,hde->qhe", query_feat, mem_m, precision=highest)
        denominator = jnp.einsum("qhd,hd->qh", query_feat, mem_z, precision=highest)
        recalled = numerator / jnp.maximum(denominator, 1.0)[..., None]
        gate_value = gate_all[first:last][None, :, None]
        combined = (
            (gate_value * recalled + (1.0 - gate_value) * local_out)
            .astype(bf16)
            .reshape(seg, group_width)
        )

        outgoing = jnp.take(combined, pslot, axis=0, mode="clip").reshape(n, cap, group_width)
        incoming = lax.all_to_all(outgoing, "ctx", 0, 0, tiled=True).reshape(slots, group_width)
        rows = jnp.take(incoming, send_slot, axis=0, mode="clip")
        gathered = lax.all_gather(rows, "head", axis=1, tiled=True)
        part = jnp.dot(
            gathered,
            weight_rows[:, first:last].reshape(head_count * group_width, out_cols),
            preferred_element_type=f32,
        )
        return part, combined

    summed, hold = one_group(0, None)
    for g in range(1, len(bounds) - 1):
        part, hold = one_group(g, hold)
        summed = summed + part
    return summed.astype(bf16)


def solution(mesh):
    return jax.shard_map(
        per_device,
        mesh=mesh,
        in_specs=(
            P("ctx", "head"),
            P("ctx", "head"),
            P("ctx", "head"),
            P(),
            P(),
            P("head"),
            P(None, "head"),
        ),
        out_specs=P("ctx", "head"),
        check_vma=False,
    )
```

```python
import jax
import jax.numpy as jnp
from jax import lax
from jax.sharding import PartitionSpec as P


def feature(inputs):
    return jax.nn.elu(inputs) + 1.0


def per_device(queries, keys, values, row_target, seg_doc, mem_gate, out_weight):
    highest = lax.Precision.HIGHEST
    f32, bf16 = jnp.float32, jnp.bfloat16
    n = lax.axis_size("ctx")
    me = lax.axis_index("ctx")
    seg, width = queries.shape
    heads = mem_gate.shape[0]
    dh = width // heads
    cap = seg // n + (seg // n) // 2
    slots = n * cap

    targets = row_target.reshape(n, seg)
    r_idx = jnp.arange(seg, dtype=jnp.int32)
    o_idx = jnp.arange(n, dtype=jnp.int32)
    s_idx = jnp.arange(slots, dtype=jnp.int32)
    w_idx = jnp.arange(cap, dtype=jnp.int32)
    lower = (r_idx[None, :] < r_idx[:, None]).astype(bf16)

    mine = lax.dynamic_index_in_dim(targets, me, 0, keepdims=False)
    owner = mine // seg
    match = (owner[:, None] == o_idx[None, :]).astype(bf16)
    before = jnp.dot(lower, match, preferred_element_type=f32)
    within = jnp.sum(jnp.where(match > 0, before, 0.0), axis=1).astype(jnp.int32)
    send_slot = owner * cap + within
    slot_row = jnp.sum(
        jnp.where(send_slot[None, :] == s_idx[:, None], r_idx[None, :], 0), axis=1
    )

    arrived = (targets // seg) == me
    rank = jnp.dot(arrived.astype(bf16), lower.T, preferred_element_type=f32).astype(jnp.int32)
    hit = arrived[:, None, :] & (rank[:, None, :] == w_idx[None, :, None])
    pslot = jnp.sum(jnp.where(hit, (targets % seg)[:, None, :], 0), axis=2).reshape(slots)
    count = jnp.sum(arrived.astype(jnp.int32), axis=1)
    valid = (w_idx[None, :] < count[:, None]).reshape(slots)
    tok_slot = jnp.sum(
        jnp.where((pslot[None, :] == r_idx[:, None]) & valid[None, :], s_idx[None, :], 0),
        axis=1,
    )

    doc = seg_doc[me]
    start = jnp.min(jnp.where(seg_doc == doc, o_idx, n))
    score_scale = dh ** (-0.5)
    causal = r_idx[:, None] >= r_idx[None, :]
    head_count = lax.axis_size("head")
    out_cols = out_weight.shape[1]
    bounds = [0, heads // 2, heads]
    weight_rows = out_weight.reshape(head_count, heads, dh, out_cols)
    gate_all = jax.nn.sigmoid(mem_gate)
    shifts = []
    step = 1
    while step < n:
        shifts.append(step)
        step *= 2

    def dispatch(source):
        buffer = jnp.take(source, slot_row, axis=0, mode="clip").reshape(n, cap, width)
        got = lax.all_to_all(buffer, "ctx", 0, 0, tiled=True).reshape(slots, width)
        return jnp.take(got, tok_slot, axis=0, mode="clip").reshape(seg, heads, dh)

    key_all = dispatch(keys)
    value_all = dispatch(values)
    query_all = dispatch(queries)

    def local_attention(query_part, key_part, value_part):
        scores = jnp.einsum(
            "qhd,khd->hqk", query_part, key_part, preferred_element_type=f32
        ) * score_scale
        scores = jnp.where(causal[None], scores, -1e30)
        row_max = jnp.max(scores, axis=-1, keepdims=True)
        weights = jnp.exp(scores - row_max)
        probabilities = (weights / jnp.sum(weights, axis=-1, keepdims=True)).astype(bf16)
        return jnp.einsum(
            "hqk,khd->qhd", probabilities, value_part, preferred_element_type=f32
        )

    def one_group(g, hold):
        first, last = bounds[g], bounds[g + 1]
        group_heads = last - first
        group_width = group_heads * dh
        cuts = [first + round(group_heads * i / len(shifts)) for i in range(len(shifts) + 1)]
        cuts = [c - first for c in cuts]
        key_heads = key_all[:, first:last]
        value_heads = value_all[:, first:last]
        query_heads = query_all[:, first:last]

        key_feat = feature(key_heads.astype(f32))
        delta_m = jnp.einsum(
            "khd,khe->hde", key_feat, value_heads.astype(f32), precision=highest
        )
        delta_z = jnp.sum(key_feat, axis=0)
        delta = jnp.concatenate([delta_m, delta_z[:, None, :]], axis=1)

        pieces = []
        total = delta
        for k, step in enumerate(shifts):
            lo, hi = cuts[k], cuts[k + 1]
            total, operands = lax.optimization_barrier(
                (total, (query_heads[:, lo:hi], key_heads[:, lo:hi], value_heads[:, lo:hi]))
            )
            perm = [(j, j + step) for j in range(n - step)]
            got = lax.ppermute(total, "ctx", perm)
            if hi > lo:
                piece = local_attention(*operands)
                got, piece = lax.optimization_barrier((got, piece))
                pieces.append(piece)
            total = total + jnp.where(me - step >= start, got, jnp.zeros_like(got))
        local_out = jnp.concatenate(pieces, axis=1)
        memory = total - delta
        mem_m = memory[:, :dh, :]
        mem_z = memory[:, dh, :]

        query_feat = feature(query_heads.astype(f32))
        numerator = jnp.einsum("qhd,hde->qhe", query_feat, mem_m, precision=highest)
        denominator = jnp.einsum("qhd,hd->qh", query_feat, mem_z, precision=highest)
        recalled = numerator / jnp.maximum(denominator, 1.0)[..., None]
        gate_value = gate_all[first:last][None, :, None]
        combined = (
            (gate_value * recalled + (1.0 - gate_value) * local_out)
            .astype(bf16)
            .reshape(seg, group_width)
        )

        outgoing = jnp.take(combined, pslot, axis=0, mode="clip").reshape(n, cap, group_width)
        incoming = lax.all_to_all(outgoing, "ctx", 0, 0, tiled=True).reshape(slots, group_width)
        rows = jnp.take(incoming, send_slot, axis=0, mode="clip")
        gathered = lax.all_gather(rows, "head", axis=1, tiled=True)
        part = jnp.dot(
            gathered,
            weight_rows[:, first:last].reshape(head_count * group_width, out_cols),
            preferred_element_type=f32,
        )
        return part, combined

    summed, hold = one_group(0, None)
    for g in range(1, len(bounds) - 1):
        part, hold = one_group(g, hold)
        summed = summed + part
    return summed.astype(bf16)


def solution(mesh):
    return jax.shard_map(
        per_device,
        mesh=mesh,
        in_specs=(
            P("ctx", "head"),
            P("ctx", "head"),
            P("ctx", "head"),
            P(),
            P(),
            P("head"),
            P(None, "head"),
        ),
        out_specs=P("ctx", "head"),
        check_vma=False,
    )
```

```python
import jax
import jax.numpy as jnp
from jax import lax
from jax.sharding import PartitionSpec as P


def feature(inputs):
    return jax.nn.elu(inputs) + 1.0


def per_device(queries, keys, values, row_target, seg_doc, mem_gate, out_weight):
    highest = lax.Precision.HIGHEST
    f32, bf16 = jnp.float32, jnp.bfloat16
    n = lax.axis_size("ctx")
    me = lax.axis_index("ctx")
    seg, width = queries.shape
    heads = mem_gate.shape[0]
    dh = width // heads
    cap = seg // n + (seg // n) // 2
    slots = n * cap

    targets = row_target.reshape(n, seg)
    r_idx = jnp.arange(seg, dtype=jnp.int32)
    o_idx = jnp.arange(n, dtype=jnp.int32)
    s_idx = jnp.arange(slots, dtype=jnp.int32)
    w_idx = jnp.arange(cap, dtype=jnp.int32)
    lower = (r_idx[None, :] < r_idx[:, None]).astype(bf16)

    mine = lax.dynamic_index_in_dim(targets, me, 0, keepdims=False)
    owner = mine // seg
    match = (owner[:, None] == o_idx[None, :]).astype(bf16)
    before = jnp.dot(lower, match, preferred_element_type=f32)
    within = jnp.sum(jnp.where(match > 0, before, 0.0), axis=1).astype(jnp.int32)
    send_slot = owner * cap + within
    slot_row = jnp.sum(
        jnp.where(send_slot[None, :] == s_idx[:, None], r_idx[None, :], 0), axis=1
    )

    arrived = (targets // seg) == me
    rank = jnp.dot(arrived.astype(bf16), lower.T, preferred_element_type=f32).astype(jnp.int32)
    hit = arrived[:, None, :] & (rank[:, None, :] == w_idx[None, :, None])
    pslot = jnp.sum(jnp.where(hit, (targets % seg)[:, None, :], 0), axis=2).reshape(slots)
    count = jnp.sum(arrived.astype(jnp.int32), axis=1)
    valid = (w_idx[None, :] < count[:, None]).reshape(slots)
    tok_slot = jnp.sum(
        jnp.where((pslot[None, :] == r_idx[:, None]) & valid[None, :], s_idx[None, :], 0),
        axis=1,
    )

    doc = seg_doc[me]
    start = jnp.min(jnp.where(seg_doc == doc, o_idx, n))
    score_scale = dh ** (-0.5)
    causal = r_idx[:, None] >= r_idx[None, :]
    head_count = lax.axis_size("head")
    out_cols = out_weight.shape[1]
    bounds = [0, heads - (3 * heads) // 8, heads]
    weight_rows = out_weight.reshape(head_count, heads, dh, out_cols)
    gate_all = jax.nn.sigmoid(mem_gate)
    shifts = []
    step = 1
    while step < n:
        shifts.append(step)
        step *= 2

    def dispatch(source):
        buffer = jnp.take(source, slot_row, axis=0, mode="clip").reshape(n, cap, width)
        got = lax.all_to_all(buffer, "ctx", 0, 0, tiled=True).reshape(slots, width)
        return jnp.take(got, tok_slot, axis=0, mode="clip").reshape(seg, heads, dh)

    key_all = dispatch(keys)
    value_all = dispatch(values)
    query_all = dispatch(queries)

    def local_attention(query_part, key_part, value_part):
        scores = jnp.einsum(
            "qhd,khd->hqk", query_part, key_part, preferred_element_type=f32
        ) * score_scale
        scores = jnp.where(causal[None], scores, -1e30)
        row_max = jnp.max(scores, axis=-1, keepdims=True)
        weights = jnp.exp(scores - row_max)
        probabilities = (weights / jnp.sum(weights, axis=-1, keepdims=True)).astype(bf16)
        return jnp.einsum(
            "hqk,khd->qhd", probabilities, value_part, preferred_element_type=f32
        )

    def one_group(g, hold):
        first, last = bounds[g], bounds[g + 1]
        group_heads = last - first
        group_width = group_heads * dh
        cuts = [first + round(group_heads * i / len(shifts)) for i in range(len(shifts) + 1)]
        cuts = [c - first for c in cuts]
        key_heads = key_all[:, first:last]
        value_heads = value_all[:, first:last]
        query_heads = query_all[:, first:last]

        key_feat = feature(key_heads.astype(f32))
        delta_m = jnp.einsum(
            "khd,khe->hde", key_feat, value_heads.astype(f32), precision=highest
        )
        delta_z = jnp.sum(key_feat, axis=0)
        delta = jnp.concatenate([delta_m, delta_z[:, None, :]], axis=1)

        pieces = []
        total = delta
        for k, step in enumerate(shifts):
            lo, hi = cuts[k], cuts[k + 1]
            total, operands = lax.optimization_barrier(
                (total, (query_heads[:, lo:hi], key_heads[:, lo:hi], value_heads[:, lo:hi]))
            )
            perm = [(j, j + step) for j in range(n - step)]
            got = lax.ppermute(total, "ctx", perm)
            if hi > lo:
                piece = local_attention(*operands)
                got, piece = lax.optimization_barrier((got, piece))
                pieces.append(piece)
            total = total + jnp.where(me - step >= start, got, jnp.zeros_like(got))
        local_out = jnp.concatenate(pieces, axis=1)
        memory = total - delta
        mem_m = memory[:, :dh, :]
        mem_z = memory[:, dh, :]

        query_feat = feature(query_heads.astype(f32))
        numerator = jnp.einsum("qhd,hde->qhe", query_feat, mem_m, precision=highest)
        denominator = jnp.einsum("qhd,hd->qh", query_feat, mem_z, precision=highest)
        recalled = numerator / jnp.maximum(denominator, 1.0)[..., None]
        gate_value = gate_all[first:last][None, :, None]
        combined = (
            (gate_value * recalled + (1.0 - gate_value) * local_out)
            .astype(bf16)
            .reshape(seg, group_width)
        )

        outgoing = jnp.take(combined, pslot, axis=0, mode="clip").reshape(n, cap, group_width)
        incoming = lax.all_to_all(outgoing, "ctx", 0, 0, tiled=True).reshape(slots, group_width)
        rows = jnp.take(incoming, send_slot, axis=0, mode="clip")
        gathered = lax.all_gather(rows, "head", axis=1, tiled=True)
        part = jnp.dot(
            gathered,
            weight_rows[:, first:last].reshape(head_count * group_width, out_cols),
            preferred_element_type=f32,
        )
        return part, combined

    summed, hold = one_group(0, None)
    for g in range(1, len(bounds) - 1):
        part, hold = one_group(g, hold)
        summed = summed + part
    return summed.astype(bf16)


def solution(mesh):
    return jax.shard_map(
        per_device,
        mesh=mesh,
        in_specs=(
            P("ctx", "head"),
            P("ctx", "head"),
            P("ctx", "head"),
            P(),
            P(),
            P("head"),
            P(None, "head"),
        ),
        out_specs=P("ctx", "head"),
        check_vma=False,
    )
```
